32 devices in a mesh: face: 2 (over y), row: 4 (over z), col: 4 (over x, core).
Axes of the slice: x: 2, y: 2, z: 4, core: 2. Of those that a mesh axis runs over, the one named last changes fastest.
Arguments:
- state: bfloat16 [6, 256, 256, 256], P('face', 'row', 'col'), may hold values from -5 to 5
- offsets: int32 [64, 2], replicated, may hold values from -4 to 4, as said below
- links: int32 [6, 4, 3], replicated, may hold values from 0 to 5, as said below
- stencil: bfloat16 [64, 256], replicated, may hold values from -5 to 5
- gain: bfloat16 [256], replicated, may hold values from 0.25 to 1.75
- w_in: bfloat16 [256, 1024], replicated, may hold values from -0.375 to 0.375
- w_out: bfloat16 [1024, 256], replicated, may hold values from -0.1875 to 0.1875
- cotangent: bfloat16 [6, 256, 256, 256], P('face', 'row', 'col'), may hold values from -0.125 to 0.125
Outputs:
- increment: bfloat16 [6, 256, 256, 256], P('face', 'row', 'col')
- stencil_grad: float32 [64, 256], replicated
- gain_grad: float32 [256], replicated
- w_in_grad: float32 [256, 1024], replicated
- w_out_grad: float32 [1024, 256], replicated
The draws below stay inside these ranges and needn't reach their ends.
Inputs may be any that keep to these rules, and one draw needn't show every extreme that they name: The 64 rows are distinct (row, column) offsets; (4, 0), (-4, 0), (0, 4) and (0, -4) are always among them. links[g, s] = (f, t, r): side s of face g (0: row 0, 1: the last row, 2: column 0, 3: the last column) meets side t of face f, and r is 1 where positions along the shared edge run in opposite directions on the two faces, else 0. The table is that of a cube whose 6 faces are each stored in one of their eight orientations: every side meets one side of another face, and the pairing is mutual.
All inputs are finite; a program needn't handle non-finite values.
Results may differ from the reference program's by a relative error of at most 0.0058.
Values may be sent and summed in bfloat16 or wider, within the bound.
No kernel may reach another device: no remote copies, remote signals or barrier semaphores. Data moves between devices by JAX's collectives and lax.ppermute only.
A program may use at most 320 MiB of HBM per device.

```python
import math
import jax
import jax.numpy as jnp
from jax import lax

FACES = 6
NF = 256
C = 256
H = 1024
OFFS = 64
RADIUS = 4


def draw_offsets(key, part):
    box_side = 2 * RADIUS + 1
    box_cells = box_side * box_side
    ranking = jax.random.permutation(key, box_cells).astype(jnp.int32)
    positions = jnp.arange(box_cells, dtype=jnp.int32)
    row_offset = positions // box_side - RADIUS
    col_offset = positions % box_side - RADIUS
    forced = (jnp.abs(row_offset) == RADIUS) & (col_offset == 0) | (jnp.abs(col_offset) == RADIUS) & (row_offset == 0)
    scores = jnp.where(forced, ranking - box_cells, ranking)
    chosen = jnp.argsort(scores, stable=True)[:OFFS]
    return jnp.stack([row_offset[chosen], col_offset[chosen]], axis=1).astype(jnp.int32)


def draw_links(key, part):
    key_order, key_row, key_col = jax.random.split(key, 3)
    directions = jnp.array([[1, 0, 0], [-1, 0, 0], [0, 1, 0], [0, -1, 0], [0, 0, 1], [0, 0, -1]], dtype=jnp.int32)
    face_order = jax.random.permutation(key_order, 6).astype(jnp.int32)
    normals = directions[face_order]
    upright = (jnp.sum(normals[:, None, :] * directions[None, :, :], axis=-1) == 0).astype(jnp.int32)
    row_pick = jax.random.randint(key_row, (6,), 0, 4)
    row_rank = jnp.cumsum(upright, axis=1) - 1
    row_choose = upright * (row_rank == row_pick[:, None]).astype(jnp.int32)
    row_axis = jnp.sum(row_choose[:, :, None] * directions[None, :, :], axis=1)
    second = upright * (jnp.sum(row_axis[:, None, :] * directions[None, :, :], axis=-1) == 0).astype(jnp.int32)
    col_pick = jax.random.randint(key_col, (6,), 0, 2)
    col_rank = jnp.cumsum(second, axis=1) - 1
    col_choose = second * (col_rank == col_pick[:, None]).astype(jnp.int32)
    col_axis = jnp.sum(col_choose[:, :, None] * directions[None, :, :], axis=1)
    side_dirs = jnp.stack([-row_axis, row_axis, -col_axis, col_axis], axis=1)
    along_axis = jnp.stack([col_axis, col_axis, row_axis, row_axis], axis=1)
    face_match = jnp.all(side_dirs[:, :, None, :] == normals[None, None, :, :], axis=-1).astype(jnp.int32)
    partner = jnp.sum(face_match * jnp.arange(6, dtype=jnp.int32), axis=-1)
    partner_dirs = jnp.sum(face_match[:, :, :, None, None] * side_dirs[None, None, :, :, :], axis=2)
    side_match = jnp.all(partner_dirs == normals[:, None, None, :], axis=-1).astype(jnp.int32)
    partner_side = jnp.sum(side_match * jnp.arange(4, dtype=jnp.int32), axis=-1)
    partner_along = jnp.sum(face_match[:, :, :, None, None] * along_axis[None, None, :, :, :], axis=2)
    partner_along = jnp.sum(side_match[:, :, :, None] * partner_along, axis=2)
    opposite = (jnp.sum(partner_along * along_axis, axis=-1) < 0).astype(jnp.int32)
    return jnp.stack([partner, partner_side, opposite], axis=-1).astype(jnp.int32)


def draw_stencil(key, part):
    key_base, key_scale = jax.random.split(key)
    base_values = jnp.clip(jax.random.normal(key_base, (OFFS, C), jnp.float32), -4.0, 4.0)
    channel_scale = jnp.exp(jax.random.uniform(key_scale, (1, C), jnp.float32, 0.0, math.log(10.0)))
    return (base_values * channel_scale * 0.125).astype(jnp.bfloat16)


def levels(rng, dims, pieces, least, largest):
    factor_of = 1.0
    for axis_at, shards_of in pieces:
        steps = jax.random.uniform(jax.random.fold_in(jax.random.fold_in(rng, 6), axis_at), (shards_of,), jnp.float32, least / len(pieces), largest / len(pieces))
        factor_of = factor_of * jnp.repeat(jnp.exp(steps), dims[axis_at] // shards_of).reshape((-1,) + (1,) * (len(dims) - 1 - axis_at))
    return factor_of


def centred(rng, dims, spread, bound, cuts=(), held_as=jnp.bfloat16):
    drawn = jax.random.normal(rng, dims, jnp.float32) * spread
    if len(cuts) > 0:
        drawn = levels(rng, dims, cuts, -0.22, 0.18) * drawn
    return jnp.clip(drawn, min=-bound, max=bound).astype(held_as)


def setup_inputs(seed: int = 0) -> dict:
    streams_of = jax.random.split(jax.random.key(seed), 9)
    state = centred(streams_of[0], (FACES, NF, NF, C), 1.0, 5.0, ((0, 2), (1, 4), (2, 4)))
    offsets = draw_offsets(jax.random.fold_in(streams_of[8], 71), 0)
    links = draw_links(jax.random.fold_in(streams_of[8], 71), 0)
    stencil = draw_stencil(jax.random.fold_in(streams_of[8], 71), 0)
    gain = jnp.clip(1.0 + 0.15 * jax.random.normal(streams_of[4], (C,), jnp.float32), 0.25, 1.75).astype(jnp.bfloat16)
    w_in = centred(streams_of[5], (C, H), C ** -0.5, 0.375)
    w_out = centred(streams_of[6], (H, C), H ** -0.5, 0.1875)
    cotangent = centred(streams_of[7], (FACES, NF, NF, C), (2.0 / NF), 0.125, ((0, 2), (1, 4), (2, 4)))
    return {"state": state, "offsets": offsets, "links": links, "stencil": stencil, "gain": gain, "w_in": w_in, "w_out": w_out, "cotangent": cotangent}


EPSILON = 1e-05

def side_strips(face_cells):
    top_strip = face_cells[:RADIUS]
    bottom_strip = jnp.flip(face_cells, 0)[:RADIUS]
    left_strip = jnp.swapaxes(face_cells[:, :RADIUS], 0, 1)
    right_strip = jnp.swapaxes(jnp.flip(face_cells, 1)[:, :RADIUS], 0, 1)
    return jnp.stack([top_strip, bottom_strip, left_strip, right_strip])

def extend(state, links):
    strips = jax.vmap(side_strips)(state)
    extended_faces = []
    for face_id in range(FACES):
        padded = jnp.pad(state[face_id], ((RADIUS, RADIUS), (RADIUS, RADIUS), (0, 0)))
        partner_strips = []
        for side_index in range(4):
            chosen = strips[links[face_id, side_index, 0], links[face_id, side_index, 1]]
            chosen = jnp.where(links[face_id, side_index, 2] == 1, jnp.flip(chosen, axis=1), chosen)
            partner_strips.append(chosen)
        padded = padded.at[:RADIUS, RADIUS:RADIUS + NF].set(jnp.flip(partner_strips[0], 0))
        padded = padded.at[RADIUS + NF:, RADIUS:RADIUS + NF].set(partner_strips[1])
        padded = padded.at[RADIUS:RADIUS + NF, :RADIUS].set(jnp.swapaxes(jnp.flip(partner_strips[2], 0), 0, 1))
        padded = padded.at[RADIUS:RADIUS + NF, RADIUS + NF:].set(jnp.swapaxes(partner_strips[3], 0, 1))
        extended_faces.append(padded)
    return jnp.stack(extended_faces)

def reference(state, offsets, links, stencil, gain, w_in, w_out, cotangent):
    extended = extend(state, links)
    rows_block = NF // 8
    weights = stencil.astype(jnp.float32)
    gain_float = gain.astype(jnp.float32)
    zero_index = jnp.zeros((), jnp.int32)

    def one_block(block_item):
        face_id = (block_item // 8).astype(jnp.int32)
        first_row = (block_item % 8 * rows_block).astype(jnp.int32)
        window = lax.dynamic_slice(extended, (face_id, first_row, zero_index, zero_index), (1, rows_block + 2 * RADIUS, NF + 2 * RADIUS, C))[0]
        target = lax.dynamic_slice(cotangent, (face_id, first_row, zero_index, zero_index), (1, rows_block, NF, C))[0]
        target_rows = target.reshape(-1, C)

        def shifted(tap_index):
            row_shift = (offsets[tap_index, 0] + RADIUS).astype(jnp.int32)
            col_shift = (offsets[tap_index, 1] + RADIUS).astype(jnp.int32)
            return lax.dynamic_slice(window, (row_shift, col_shift, zero_index), (rows_block, NF, C)).astype(jnp.float32)

        def add_tap(tap_index, running):
            return running + weights[tap_index] * shifted(tap_index)
        aggregated = lax.fori_loop(0, OFFS, add_tap, jnp.zeros((rows_block, NF, C), jnp.float32)).reshape(-1, C)
        mean_square = lax.optimization_barrier(jnp.mean(aggregated * aggregated, axis=-1, keepdims=True))
        inverse_rms = lax.rsqrt(mean_square + EPSILON)
        normalized = aggregated * inverse_rms
        hidden_in = (normalized * gain_float).astype(jnp.bfloat16)
        pre_act = jnp.dot(hidden_in, w_in, preferred_element_type=jnp.float32)
        sigmoid_pre = jax.nn.sigmoid(pre_act)
        activated = (pre_act * sigmoid_pre).astype(jnp.bfloat16)
        increment = jnp.dot(activated, w_out, preferred_element_type=jnp.float32).astype(jnp.bfloat16)
        w_out_grad = jnp.dot(activated.T, target_rows, preferred_element_type=jnp.float32)
        act_grad = jnp.dot(target_rows, w_out.T, preferred_element_type=jnp.float32)
        pre_grad = (act_grad * sigmoid_pre * (1.0 + pre_act * (1.0 - sigmoid_pre))).astype(jnp.bfloat16)
        w_in_grad = jnp.dot(hidden_in.T, pre_grad, preferred_element_type=jnp.float32)
        hidden_grad = jnp.dot(pre_grad, w_in.T, preferred_element_type=jnp.float32)
        gain_grad = lax.optimization_barrier(jnp.sum(hidden_grad * normalized, axis=0))
        scaled_grad = hidden_grad * gain_float
        aggregated_grad = inverse_rms * (scaled_grad - normalized * lax.optimization_barrier(jnp.mean(scaled_grad * normalized, axis=-1, keepdims=True)))
        aggregated_grad = aggregated_grad.reshape(rows_block, NF, C)

        def tap_grad(tap_index):
            return lax.optimization_barrier(jnp.sum(aggregated_grad * shifted(tap_index), axis=(0, 1)))
        stencil_grad = lax.map(tap_grad, jnp.arange(OFFS, dtype=jnp.int32))
        return (increment.reshape(rows_block, NF, C), stencil_grad, gain_grad, w_in_grad, w_out_grad)
    outputs = lax.map(one_block, jnp.arange(FACES * 8, dtype=jnp.int32))
    increment = outputs[0].reshape(FACES, NF, NF, C)
    return (increment, lax.optimization_barrier(jnp.sum(outputs[1], axis=0)), lax.optimization_barrier(jnp.sum(outputs[2], axis=0)), lax.optimization_barrier(jnp.sum(outputs[3], axis=0)), lax.optimization_barrier(jnp.sum(outputs[4], axis=0)))
```

```python
import jax
import jax.numpy as jnp
from jax import lax
from jax.experimental import pallas as pl
from jax.experimental.pallas import tpu as pltpu
from jax.sharding import PartitionSpec as P

RADIUS = 4
BOX = 2 * RADIUS + 1


def _fwd_kernel(ext_ref, w_ref, out_ref, shift_ref):
    rows = out_ref.shape[1]
    cols = out_ref.shape[2]
    ext_rows = ext_ref.shape[1]
    for dj in range(BOX):
        def shift_row(r, carry):
            shift_ref[r] = ext_ref[0, r, pl.ds(dj, cols), :].astype(jnp.float32)
            return carry

        lax.fori_loop(0, ext_rows, shift_row, 0)
        weights = [w_ref[pl.ds(di * BOX + dj, 1), :] for di in range(BOX)]

        def out_row(i, carry):
            if dj == 0:
                acc = jnp.zeros((cols, out_ref.shape[3]), jnp.float32)
            else:
                acc = out_ref[0, i]
            for di in range(BOX):
                acc = acc + weights[di] * shift_ref[i + di]
            out_ref[0, i] = acc
            return carry

        lax.fori_loop(0, rows, out_row, 0)


def _bwd_kernel(ext_ref, g_ref, out_ref, shift_ref):
    rows = g_ref.shape[1]
    cols = g_ref.shape[2]
    chans = g_ref.shape[3]
    ext_rows = ext_ref.shape[1]

    @pl.when(pl.program_id(0) == 0)
    def _():
        out_ref[...] = jnp.zeros_like(out_ref)

    for dj in range(BOX):
        def shift_row(r, carry):
            shift_ref[r] = ext_ref[0, r, pl.ds(dj, cols), :].astype(jnp.float32)
            return carry

        lax.fori_loop(0, ext_rows, shift_row, 0)

        def grad_row(i, accs):
            g = g_ref[0, i]
            new = []
            for di in range(BOX):
                p = g * shift_ref[i + di]
                p = p.reshape(cols // 8, 8, chans).sum(axis=0)
                new.append(accs[di] + p)
            return tuple(new)

        init = tuple(jnp.zeros((8, chans), jnp.float32) for _ in range(BOX))
        accs = lax.fori_loop(0, rows, grad_row, init)
        for di in range(BOX):
            out_ref[di * BOX + dj] = out_ref[di * BOX + dj] + accs[di]


def stencil_forward(ext, box_weights):
    faces, ext_rows, ext_cols, chans = ext.shape
    rows = ext_rows - 2 * RADIUS
    cols = ext_cols - 2 * RADIUS
    return pl.pallas_call(
        _fwd_kernel,
        grid=(faces,),
        in_specs=[
            pl.BlockSpec((1, ext_rows, ext_cols, chans), lambda f: (f, 0, 0, 0)),
            pl.BlockSpec((BOX * BOX, chans), lambda f: (0, 0)),
        ],
        out_specs=pl.BlockSpec((1, rows, cols, chans), lambda f: (f, 0, 0, 0)),
        out_shape=jax.ShapeDtypeStruct((faces, rows, cols, chans), jnp.float32),
        scratch_shapes=[pltpu.VMEM((ext_rows, cols, chans), jnp.float32)],
        compiler_params=pltpu.CompilerParams(
            dimension_semantics=("arbitrary",), vmem_limit_bytes=48 * 1024 * 1024
        ),
    )(ext, box_weights)


def stencil_backward(ext, agg_grad):
    faces, ext_rows, ext_cols, chans = ext.shape
    rows = ext_rows - 2 * RADIUS
    cols = ext_cols - 2 * RADIUS
    partial = pl.pallas_call(
        _bwd_kernel,
        grid=(faces,),
        in_specs=[
            pl.BlockSpec((1, ext_rows, ext_cols, chans), lambda f: (f, 0, 0, 0)),
            pl.BlockSpec((1, rows, cols, chans), lambda f: (f, 0, 0, 0)),
        ],
        out_specs=pl.BlockSpec((BOX * BOX, 8, chans), lambda f: (0, 0, 0)),
        out_shape=jax.ShapeDtypeStruct((BOX * BOX, 8, chans), jnp.float32),
        scratch_shapes=[pltpu.VMEM((ext_rows, cols, chans), jnp.float32)],
        compiler_params=pltpu.CompilerParams(
            dimension_semantics=("arbitrary",), vmem_limit_bytes=48 * 1024 * 1024
        ),
    )(ext, agg_grad)
    return jnp.sum(partial, axis=1)


def with_halo(cells, sides, width):
    for axis, dim in sides:
        count = lax.axis_size(axis)
        ends = count - 1
        head = lax.slice_in_dim(cells, 0, width, axis=dim)
        tail = lax.slice_in_dim(cells, cells.shape[dim] - width, cells.shape[dim], axis=dim)
        cells = jnp.concatenate(
            [
                lax.ppermute(tail, axis, [(i, (i + 1) % count) for i in range(ends)]),
                cells,
                lax.ppermute(head, axis, [((i + 1) % count, i) for i in range(ends)]),
            ],
            axis=dim,
        )
    return cells


def cut_segment(padded_edges, face_local, side_index, flip_flag, start_cell, length):
    padded_len = padded_edges.shape[3]
    begin_cell = jnp.where(flip_flag == 1, padded_len - start_cell - length, start_cell)
    zero_index = jnp.zeros((), jnp.int32)
    segment = lax.dynamic_slice(
        padded_edges,
        (face_local, side_index, zero_index, begin_cell, zero_index),
        (1, 1, padded_edges.shape[2], length, padded_edges.shape[4]),
    )[0, 0]
    return jnp.where(flip_flag == 1, jnp.flip(segment, axis=1), segment)


def shards(state, offsets, links, stencil, gain, w_in, w_out, cotangent):
    local_count, rows_dev, cols_dev, channels = state.shape
    row_count = lax.axis_size("row")
    col_count = lax.axis_size("col")
    face_count = lax.axis_size("face")
    face_side = rows_dev * row_count
    piece_cells = face_side // (row_count * col_count)
    row_index = lax.axis_index("row")
    col_index = lax.axis_index("col")
    face_index = lax.axis_index("face")
    radius_cells = RADIUS
    extended = with_halo(state, (("row", 1), ("col", 2)), RADIUS)
    top_strip = state[:, :radius_cells]
    bottom_strip = jnp.flip(state[:, rows_dev - radius_cells :], axis=1)
    left_strip = jnp.swapaxes(state[:, :, :radius_cells], 1, 2)
    right_strip = jnp.swapaxes(jnp.flip(state[:, :, cols_dev - radius_cells :], axis=2), 1, 2)
    across = jnp.where(row_index == 0, top_strip, bottom_strip)
    downward = jnp.where(col_index == 0, left_strip, right_strip)
    across_pieces = jnp.moveaxis(
        across.reshape(local_count, radius_cells, row_count, piece_cells, channels), 2, 0
    )
    down_pieces = jnp.moveaxis(
        downward.reshape(local_count, radius_cells, col_count, piece_cells, channels), 2, 0
    )
    empty_slots = jnp.zeros(
        (row_count * col_count, local_count, radius_cells, piece_cells, channels), state.dtype
    )
    across_slots = lax.dynamic_update_slice_in_dim(
        empty_slots, across_pieces, col_index * row_count, 0
    )
    down_slots = lax.dynamic_update_slice_in_dim(empty_slots, down_pieces, row_index * col_count, 0)
    outgoing = jnp.stack([across_slots, down_slots], axis=2).reshape(
        row_count, col_count, local_count, 2, radius_cells, piece_cells, channels
    )
    arrived = lax.all_to_all(
        lax.all_to_all(outgoing, "row", split_axis=0, concat_axis=0, tiled=True),
        "col",
        split_axis=1,
        concat_axis=1,
        tiled=True,
    )
    own_pieces = jnp.stack(
        [
            jnp.sum(arrived[0, :, :, 0], axis=0),
            jnp.sum(arrived[row_count - 1, :, :, 0], axis=0),
            jnp.sum(arrived[:, 0, :, 1], axis=0),
            jnp.sum(arrived[:, col_count - 1, :, 1], axis=0),
        ],
        axis=1,
    )
    across_side = jnp.where(row_index == 0, 0, 1).astype(jnp.int32)
    down_side = jnp.where(col_index == 0, 2, 3).astype(jnp.int32)
    across_len = cols_dev + 2 * radius_cells
    down_len = rows_dev + 2 * radius_cells
    edge_pad = ((0, 0), (0, 0), (0, 0), (radius_cells, radius_cells), (0, 0))
    side_edges = lax.all_gather(own_pieces, ("row", "col"), axis=3, tiled=True)
    padded_edges = jnp.pad(side_edges, edge_pad)
    across_list = []
    down_list = []
    for dest_face in range(local_count * face_count):
        link_across = lax.dynamic_index_in_dim(links[dest_face], across_side, 0, keepdims=False)
        link_down = lax.dynamic_index_in_dim(links[dest_face], down_side, 0, keepdims=False)
        segment_across = cut_segment(
            padded_edges,
            link_across[0] % local_count,
            link_across[1],
            link_across[2],
            col_index * cols_dev,
            across_len,
        )
        segment_down = cut_segment(
            padded_edges,
            link_down[0] % local_count,
            link_down[1],
            link_down[2],
            row_index * rows_dev,
            down_len,
        )
        across_list.append(
            jnp.where(
                link_across[0] // local_count == face_index,
                segment_across,
                jnp.zeros_like(segment_across),
            )
        )
        down_list.append(
            jnp.where(
                link_down[0] // local_count == face_index,
                segment_down,
                jnp.zeros_like(segment_down),
            )
        )
    got_across, got_down = (
        lax.all_to_all(jnp.stack(across_list), "face", split_axis=0, concat_axis=0, tiled=True),
        lax.all_to_all(jnp.stack(down_list), "face", split_axis=0, concat_axis=0, tiled=True),
    )
    halo_across = jnp.sum(
        got_across.reshape(face_count, local_count, radius_cells, across_len, channels), axis=0
    )
    halo_down = jnp.sum(
        got_down.reshape(face_count, local_count, radius_cells, down_len, channels), axis=0
    )
    top_part = jnp.where(row_index == 0, jnp.flip(halo_across, axis=1), jnp.zeros_like(halo_across))
    bottom_part = jnp.where(row_index == row_count - 1, halo_across, jnp.zeros_like(halo_across))
    left_block = jnp.swapaxes(jnp.flip(halo_down, axis=1), 1, 2)
    right_block = jnp.swapaxes(halo_down, 1, 2)
    left_part = jnp.where(col_index == 0, left_block, jnp.zeros_like(left_block))
    right_part = jnp.where(col_index == col_count - 1, right_block, jnp.zeros_like(right_block))
    extended = extended.at[:, :radius_cells].add(top_part)
    extended = extended.at[:, radius_cells + rows_dev :].add(bottom_part)
    extended = extended.at[:, :, :radius_cells].add(left_part)
    extended = extended.at[:, :, radius_cells + cols_dev :].add(right_part)
    box_side = 2 * radius_cells + 1
    box_index = (offsets[:, 0] + radius_cells) * box_side + offsets[:, 1] + radius_cells
    onehot = (
        box_index[:, None] == jnp.arange(box_side * box_side, dtype=jnp.int32)[None, :]
    ).astype(jnp.float32)
    box_weights = jnp.dot(onehot.T, stencil.astype(jnp.float32), precision=lax.Precision.HIGHEST)
    aggregated = stencil_forward(extended, box_weights)
    cell_count = local_count * rows_dev * cols_dev
    aggregated = aggregated.reshape(cell_count, channels)
    mean_square = jnp.mean(aggregated * aggregated, axis=-1, keepdims=True)
    inverse_rms = lax.rsqrt(mean_square + 1e-05)
    normalized = aggregated * inverse_rms
    gain_float = gain.astype(jnp.float32)
    hidden_in = (normalized * gain_float).astype(jnp.bfloat16)
    pre_act = jnp.dot(hidden_in, w_in, preferred_element_type=jnp.float32)
    sigmoid_pre = jax.nn.sigmoid(pre_act)
    activated = (pre_act * sigmoid_pre).astype(jnp.bfloat16)
    increment = jnp.dot(activated, w_out, preferred_element_type=jnp.float32).astype(jnp.bfloat16)
    target_rows = cotangent.reshape(cell_count, channels)
    contract_rows = (((0,), (0,)), ((), ()))
    contract_cols = (((1,), (1,)), ((), ()))
    w_out_grad = lax.dot_general(
        activated, target_rows, contract_rows, preferred_element_type=jnp.float32
    )
    w_out_grad = lax.psum(w_out_grad, ("face", "row", "col"))
    act_grad = lax.dot_general(
        target_rows, w_out, contract_cols, preferred_element_type=jnp.float32
    )
    pre_grad = (act_grad * sigmoid_pre * (1.0 + pre_act * (1.0 - sigmoid_pre))).astype(jnp.bfloat16)
    w_in_grad = lax.dot_general(
        hidden_in, pre_grad, contract_rows, preferred_element_type=jnp.float32
    )
    w_in_grad = lax.psum(w_in_grad, ("face", "row", "col"))
    hidden_grad = lax.dot_general(pre_grad, w_in, contract_cols, preferred_element_type=jnp.float32)
    gain_grad = jnp.sum(hidden_grad * normalized, axis=0)
    scaled_grad = hidden_grad * gain_float
    aggregated_grad = inverse_rms * (
        scaled_grad - normalized * jnp.mean(scaled_grad * normalized, axis=-1, keepdims=True)
    )
    aggregated_grad = aggregated_grad.reshape(local_count, rows_dev, cols_dev, channels)
    box_grads = stencil_backward(extended, aggregated_grad)
    stencil_grad = jnp.dot(onehot, box_grads, precision=lax.Precision.HIGHEST)
    stencil_grad, gain_grad, w_in_grad, w_out_grad = lax.optimization_barrier(
        (stencil_grad, gain_grad, w_in_grad, w_out_grad)
    )
    summed = lax.psum((stencil_grad, gain_grad), ("face", "row", "col"))
    return (increment.reshape(state.shape), summed[0], summed[1], w_in_grad, w_out_grad)


def solution(mesh):
    in_specs = (
        P("face", "row", "col", None),
        P(),
        P(),
        P(),
        P(),
        P(),
        P(),
        P("face", "row", "col", None),
    )
    out_specs = (P("face", "row", "col", None), P(), P(), P(), P())
    return jax.shard_map(shards, mesh=mesh, in_specs=in_specs, out_specs=out_specs, check_vma=False)
```

```python
import jax
import jax.numpy as jnp
from jax import lax
from jax.experimental import pallas as pl
from jax.experimental.pallas import tpu as pltpu
from jax.sharding import PartitionSpec as P

RADIUS = 4
BOX = 2 * RADIUS + 1


def _fwd_kernel(ext_ref, w_ref, out_ref, shift_ref):
    rows = out_ref.shape[1]
    cols = out_ref.shape[2]
    ext_rows = ext_ref.shape[1]
    for dj in range(BOX):
        def shift_row(r, carry):
            shift_ref[r] = ext_ref[0, r, pl.ds(dj, cols), :].astype(jnp.float32)
            return carry

        lax.fori_loop(0, ext_rows, shift_row, 0)
        weights = [w_ref[pl.ds(di * BOX + dj, 1), :] for di in range(BOX)]

        def out_row(i, carry):
            if dj == 0:
                acc = jnp.zeros((cols, out_ref.shape[3]), jnp.float32)
            else:
                acc = out_ref[0, i]
            for di in range(BOX):
                acc = acc + weights[di] * shift_ref[i + di]
            out_ref[0, i] = acc
            return carry

        lax.fori_loop(0, rows, out_row, 0)


def _bwd_kernel(ext_ref, g_ref, out_ref, shift_ref):
    rows = g_ref.shape[1]
    cols = g_ref.shape[2]
    chans = g_ref.shape[3]
    ext_rows = ext_ref.shape[1]

    @pl.when(pl.program_id(0) == 0)
    def _():
        out_ref[...] = jnp.zeros_like(out_ref)

    for dj in range(BOX):
        def shift_row(r, carry):
            shift_ref[r] = ext_ref[0, r, pl.ds(dj, cols), :].astype(jnp.float32)
            return carry

        lax.fori_loop(0, ext_rows, shift_row, 0)

        def grad_row(i, accs):
            g = g_ref[0, i]
            new = []
            for di in range(BOX):
                p = g * shift_ref[i + di]
                p = p.reshape(cols // 8, 8, chans).sum(axis=0)
                new.append(accs[di] + p)
            return tuple(new)

        init = tuple(jnp.zeros((8, chans), jnp.float32) for _ in range(BOX))
        accs = lax.fori_loop(0, rows, grad_row, init)
        for di in range(BOX):
            out_ref[di * BOX + dj] = out_ref[di * BOX + dj] + accs[di]


def stencil_forward(ext, box_weights):
    faces, ext_rows, ext_cols, chans = ext.shape
    rows = ext_rows - 2 * RADIUS
    cols = ext_cols - 2 * RADIUS
    return pl.pallas_call(
        _fwd_kernel,
        grid=(faces,),
        in_specs=[
            pl.BlockSpec((1, ext_rows, ext_cols, chans), lambda f: (f, 0, 0, 0)),
            pl.BlockSpec((BOX * BOX, chans), lambda f: (0, 0)),
        ],
        out_specs=pl.BlockSpec((1, rows, cols, chans), lambda f: (f, 0, 0, 0)),
        out_shape=jax.ShapeDtypeStruct((faces, rows, cols, chans), jnp.float32),
        scratch_shapes=[pltpu.VMEM((ext_rows, cols, chans), jnp.float32)],
        compiler_params=pltpu.CompilerParams(
            dimension_semantics=("arbitrary",), vmem_limit_bytes=48 * 1024 * 1024
        ),
    )(ext, box_weights)


def stencil_backward(ext, agg_grad):
    faces, ext_rows, ext_cols, chans = ext.shape
    rows = ext_rows - 2 * RADIUS
    cols = ext_cols - 2 * RADIUS
    partial = pl.pallas_call(
        _bwd_kernel,
        grid=(faces,),
        in_specs=[
            pl.BlockSpec((1, ext_rows, ext_cols, chans), lambda f: (f, 0, 0, 0)),
            pl.BlockSpec((1, rows, cols, chans), lambda f: (f, 0, 0, 0)),
        ],
        out_specs=pl.BlockSpec((BOX * BOX, 8, chans), lambda f: (0, 0, 0)),
        out_shape=jax.ShapeDtypeStruct((BOX * BOX, 8, chans), jnp.float32),
        scratch_shapes=[pltpu.VMEM((ext_rows, cols, chans), jnp.float32)],
        compiler_params=pltpu.CompilerParams(
            dimension_semantics=("arbitrary",), vmem_limit_bytes=48 * 1024 * 1024
        ),
    )(ext, agg_grad)
    return jnp.sum(partial, axis=1)


def with_halo(cells, sides, width):
    for axis, dim in sides:
        count = lax.axis_size(axis)
        ends = count - 1
        head = lax.slice_in_dim(cells, 0, width, axis=dim)
        tail = lax.slice_in_dim(cells, cells.shape[dim] - width, cells.shape[dim], axis=dim)
        cells = jnp.concatenate(
            [
                lax.ppermute(tail, axis, [(i, (i + 1) % count) for i in range(ends)]),
                cells,
                lax.ppermute(head, axis, [((i + 1) % count, i) for i in range(ends)]),
            ],
            axis=dim,
        )
    return cells


def cut_segment(padded_edges, face_local, side_index, flip_flag, start_cell, length):
    padded_len = padded_edges.shape[3]
    begin_cell = jnp.where(flip_flag == 1, padded_len - start_cell - length, start_cell)
    zero_index = jnp.zeros((), jnp.int32)
    segment = lax.dynamic_slice(
        padded_edges,
        (face_local, side_index, zero_index, begin_cell, zero_index),
        (1, 1, padded_edges.shape[2], length, padded_edges.shape[4]),
    )[0, 0]
    return jnp.where(flip_flag == 1, jnp.flip(segment, axis=1), segment)


def shards(state, offsets, links, stencil, gain, w_in, w_out, cotangent):
    local_count, rows_dev, cols_dev, channels = state.shape
    row_count = lax.axis_size("row")
    col_count = lax.axis_size("col")
    face_count = lax.axis_size("face")
    face_side = rows_dev * row_count
    piece_cells = face_side // (row_count * col_count)
    row_index = lax.axis_index("row")
    col_index = lax.axis_index("col")
    face_index = lax.axis_index("face")
    radius_cells = RADIUS
    extended = with_halo(state, (("row", 1), ("col", 2)), RADIUS)
    top_strip = state[:, :radius_cells]
    bottom_strip = jnp.flip(state[:, rows_dev - radius_cells :], axis=1)
    left_strip = jnp.swapaxes(state[:, :, :radius_cells], 1, 2)
    right_strip = jnp.swapaxes(jnp.flip(state[:, :, cols_dev - radius_cells :], axis=2), 1, 2)
    across = jnp.where(row_index == 0, top_strip, bottom_strip)
    downward = jnp.where(col_index == 0, left_strip, right_strip)
    sub_across = cols_dev // row_count
    sub_down = rows_dev // col_count
    across_sub = lax.all_to_all(
        across.reshape(local_count, radius_cells, row_count, sub_across, channels),
        "row",
        split_axis=2,
        concat_axis=2,
        tiled=True,
    )
    down_sub = lax.all_to_all(
        downward.reshape(local_count, radius_cells, col_count, sub_down, channels),
        "col",
        split_axis=2,
        concat_axis=2,
        tiled=True,
    )
    own_across = jnp.stack([across_sub[:, :, 0], across_sub[:, :, row_count - 1]], axis=1)
    own_down = jnp.stack([down_sub[:, :, 0], down_sub[:, :, col_count - 1]], axis=1)
    across_all = lax.all_gather(own_across, ("row", "col")).reshape(
        row_count, col_count, local_count, 2, radius_cells, sub_across, channels
    )
    down_all = lax.all_gather(own_down, ("row", "col")).reshape(
        row_count, col_count, local_count, 2, radius_cells, sub_down, channels
    )
    across_full = jnp.transpose(across_all, (2, 3, 4, 1, 0, 5, 6)).reshape(
        local_count, 2, radius_cells, face_side, channels
    )
    down_full = jnp.transpose(down_all, (2, 3, 4, 0, 1, 5, 6)).reshape(
        local_count, 2, radius_cells, face_side, channels
    )
    side_edges = jnp.concatenate([across_full, down_full], axis=1)
    across_side = jnp.where(row_index == 0, 0, 1).astype(jnp.int32)
    down_side = jnp.where(col_index == 0, 2, 3).astype(jnp.int32)
    across_len = cols_dev + 2 * radius_cells
    down_len = rows_dev + 2 * radius_cells
    edge_pad = ((0, 0), (0, 0), (0, 0), (radius_cells, radius_cells), (0, 0))
    padded_edges = jnp.pad(side_edges, edge_pad)
    across_list = []
    down_list = []
    for dest_face in range(local_count * face_count):
        link_across = lax.dynamic_index_in_dim(links[dest_face], across_side, 0, keepdims=False)
        link_down = lax.dynamic_index_in_dim(links[dest_face], down_side, 0, keepdims=False)
        segment_across = cut_segment(
            padded_edges,
            link_across[0] % local_count,
            link_across[1],
            link_across[2],
            col_index * cols_dev,
            across_len,
        )
        segment_down = cut_segment(
            padded_edges,
            link_down[0] % local_count,
            link_down[1],
            link_down[2],
            row_index * rows_dev,
            down_len,
        )
        across_list.append(
            jnp.where(
                link_across[0] // local_count == face_index,
                segment_across,
                jnp.zeros_like(segment_across),
            )
        )
        down_list.append(
            jnp.where(
                link_down[0] // local_count == face_index,
                segment_down,
                jnp.zeros_like(segment_down),
            )
        )
    got_across, got_down = (
        lax.all_to_all(jnp.stack(across_list), "face", split_axis=0, concat_axis=0, tiled=True),
        lax.all_to_all(jnp.stack(down_list), "face", split_axis=0, concat_axis=0, tiled=True),
    )
    halo_across = jnp.sum(
        got_across.reshape(face_count, local_count, radius_cells, across_len, channels), axis=0
    )
    halo_down = jnp.sum(
        got_down.reshape(face_count, local_count, radius_cells, down_len, channels), axis=0
    )
    top_part = jnp.where(row_index == 0, jnp.flip(halo_across, axis=1), jnp.zeros_like(halo_across))
    bottom_part = jnp.where(row_index == row_count - 1, halo_across, jnp.zeros_like(halo_across))
    left_block = jnp.swapaxes(jnp.flip(halo_down, axis=1), 1, 2)
    right_block = jnp.swapaxes(halo_down, 1, 2)
    left_part = jnp.where(col_index == 0, left_block, jnp.zeros_like(left_block))
    right_part = jnp.where(col_index == col_count - 1, right_block, jnp.zeros_like(right_block))
    extended = extended.at[:, :radius_cells].add(top_part)
    extended = extended.at[:, radius_cells + rows_dev :].add(bottom_part)
    extended = extended.at[:, :, :radius_cells].add(left_part)
    extended = extended.at[:, :, radius_cells + cols_dev :].add(right_part)
    box_side = 2 * radius_cells + 1
    box_index = (offsets[:, 0] + radius_cells) * box_side + offsets[:, 1] + radius_cells
    onehot = (
        box_index[:, None] == jnp.arange(box_side * box_side, dtype=jnp.int32)[None, :]
    ).astype(jnp.float32)
    box_weights = jnp.dot(onehot.T, stencil.astype(jnp.float32), precision=lax.Precision.HIGHEST)
    aggregated = stencil_forward(extended, box_weights)
    cell_count = local_count * rows_dev * cols_dev
    aggregated = aggregated.reshape(cell_count, channels)
    mean_square = jnp.mean(aggregated * aggregated, axis=-1, keepdims=True)
    inverse_rms = lax.rsqrt(mean_square + 1e-05)
    normalized = aggregated * inverse_rms
    gain_float = gain.astype(jnp.float32)
    hidden_in = (normalized * gain_float).astype(jnp.bfloat16)
    pre_act = jnp.dot(hidden_in, w_in, preferred_element_type=jnp.float32)
    sigmoid_pre = jax.nn.sigmoid(pre_act)
    activated = (pre_act * sigmoid_pre).astype(jnp.bfloat16)
    increment = jnp.dot(activated, w_out, preferred_element_type=jnp.float32).astype(jnp.bfloat16)
    target_rows = cotangent.reshape(cell_count, channels)
    contract_rows = (((0,), (0,)), ((), ()))
    contract_cols = (((1,), (1,)), ((), ()))
    w_out_grad = lax.dot_general(
        activated, target_rows, contract_rows, preferred_element_type=jnp.float32
    )
    act_grad = lax.dot_general(
        target_rows, w_out, contract_cols, preferred_element_type=jnp.float32
    )
    pre_grad = (act_grad * sigmoid_pre * (1.0 + pre_act * (1.0 - sigmoid_pre))).astype(jnp.bfloat16)
    w_in_grad = lax.dot_general(
        hidden_in, pre_grad, contract_rows, preferred_element_type=jnp.float32
    )
    hidden_grad = lax.dot_general(pre_grad, w_in, contract_cols, preferred_element_type=jnp.float32)
    gain_grad = jnp.sum(hidden_grad * normalized, axis=0)
    out_rows = w_out_grad.shape[0]
    w_in_grad, out_and_gain = lax.psum(
        (w_in_grad, jnp.concatenate([w_out_grad, gain_grad[None, :]], axis=0)),
        ("face", "row", "col"),
    )
    w_out_grad = out_and_gain[:out_rows]
    gain_grad = out_and_gain[out_rows]
    scaled_grad = hidden_grad * gain_float
    aggregated_grad = inverse_rms * (
        scaled_grad - normalized * jnp.mean(scaled_grad * normalized, axis=-1, keepdims=True)
    )
    aggregated_grad = aggregated_grad.reshape(local_count, rows_dev, cols_dev, channels)
    box_grads = stencil_backward(extended, aggregated_grad)
    stencil_grad = jnp.dot(onehot, box_grads, precision=lax.Precision.HIGHEST)
    stencil_grad, w_in_grad, out_and_gain = lax.optimization_barrier(
        (stencil_grad, w_in_grad, out_and_gain)
    )
    w_out_grad = out_and_gain[:out_rows]
    gain_grad = out_and_gain[out_rows]
    stencil_grad = butterfly_sum(stencil_grad, ("face", "row", "col"))
    return (increment.reshape(state.shape), stencil_grad, gain_grad, w_in_grad, w_out_grad)


def butterfly_sum(value, axes):
    for axis in axes:
        count = lax.axis_size(axis)
        if count & (count - 1):
            value = lax.psum(value, axis)
            continue
        step = 1
        while step < count:
            value = value + lax.ppermute(value, axis, [(i, i ^ step) for i in range(count)])
            step *= 2
    return value


def solution(mesh):
    in_specs = (
        P("face", "row", "col", None),
        P(),
        P(),
        P(),
        P(),
        P(),
        P(),
        P("face", "row", "col", None),
    )
    out_specs = (P("face", "row", "col", None), P(), P(), P(), P())
    return jax.shard_map(shards, mesh=mesh, in_specs=in_specs, out_specs=out_specs, check_vma=False)
```

```python
import jax
import jax.numpy as jnp
from jax import lax
from jax.experimental import pallas as pl
from jax.experimental.pallas import tpu as pltpu
from jax.sharding import PartitionSpec as P

RADIUS = 4
BOX = 2 * RADIUS + 1


def _fwd_kernel(ext_ref, w_ref, out_ref, shift_ref):
    rows = out_ref.shape[1]
    cols = out_ref.shape[2]
    ext_rows = ext_ref.shape[1]
    row_block = 4 if rows % 4 == 0 else 1
    for dj in range(BOX):
        def shift_row(r, carry):
            shift_ref[r] = ext_ref[0, r, pl.ds(dj, cols), :].astype(jnp.float32)
            return carry

        lax.fori_loop(0, ext_rows, shift_row, 0)
        weights = [w_ref[pl.ds(di * BOX + dj, 1), :] for di in range(BOX)]

        def out_rows(block_index, carry):
            first = block_index * row_block
            if dj == 0:
                accs = [jnp.zeros((cols, out_ref.shape[3]), jnp.float32) for _ in range(row_block)]
            else:
                accs = [out_ref[0, first + q] for q in range(row_block)]
            for t in range(BOX + row_block - 1):
                window = shift_ref[first + t]
                for q in range(row_block):
                    if 0 <= t - q < BOX:
                        accs[q] = accs[q] + weights[t - q] * window
            for q in range(row_block):
                out_ref[0, first + q] = accs[q]
            return carry

        lax.fori_loop(0, rows // row_block, out_rows, 0)


def stencil_forward(ext, box_weights):
    faces, ext_rows, ext_cols, chans = ext.shape
    rows = ext_rows - 2 * RADIUS
    cols = ext_cols - 2 * RADIUS
    return pl.pallas_call(
        _fwd_kernel,
        grid=(faces,),
        in_specs=[
            pl.BlockSpec((1, ext_rows, ext_cols, chans), lambda f: (f, 0, 0, 0)),
            pl.BlockSpec((BOX * BOX, chans), lambda f: (0, 0)),
        ],
        out_specs=pl.BlockSpec((1, rows, cols, chans), lambda f: (f, 0, 0, 0)),
        out_shape=jax.ShapeDtypeStruct((faces, rows, cols, chans), jnp.float32),
        scratch_shapes=[pltpu.VMEM((ext_rows, cols, chans), jnp.float32)],
        compiler_params=pltpu.CompilerParams(
            dimension_semantics=("arbitrary",), vmem_limit_bytes=48 * 1024 * 1024
        ),
    )(ext, box_weights)


def _fill_slabs(ext_ref, slab_ref, first_row):
    cols = slab_ref.shape[2]
    for dj in range(BOX):
        def shift_row(r, carry):
            slab_ref[dj, r] = ext_ref[0, first_row + r, pl.ds(dj, cols), :].astype(jnp.float32)
            return carry

        lax.fori_loop(0, slab_ref.shape[1], shift_row, 0)


def _bwd_kernel(off_ref, ext_ref, g_ref, out_ref, slab_ref):
    rows, cols, chans = g_ref.shape[1], g_ref.shape[2], g_ref.shape[3]
    block = slab_ref.shape[1] - 2 * RADIUS

    @pl.when(pl.program_id(0) == 0)
    def _():
        out_ref[...] = jnp.zeros_like(out_ref)

    for first_row in range(0, rows, block):
        _fill_slabs(ext_ref, slab_ref, first_row)

        def grad_row(i, carry):
            g = g_ref[0, first_row + i]
            for tap in range(out_ref.shape[0]):
                di = off_ref[2 * tap] + RADIUS
                dj = off_ref[2 * tap + 1] + RADIUS
                p = (g * slab_ref[dj, i + di]).reshape(cols // 8, 8, chans).sum(axis=0)
                out_ref[tap] = out_ref[tap] + p
            return carry

        lax.fori_loop(0, block, grad_row, 0)


def _slab_block(rows):
    block = min(rows, 32)
    while rows % block:
        block -= 1
    return block


def stencil_backward(offsets, ext, agg_grad):
    faces, ext_rows, ext_cols, chans = ext.shape
    rows = ext_rows - 2 * RADIUS
    cols = ext_cols - 2 * RADIUS
    taps = offsets.shape[0]
    block = _slab_block(rows)
    partial = pl.pallas_call(
        _bwd_kernel,
        grid_spec=pltpu.PrefetchScalarGridSpec(
            num_scalar_prefetch=1,
            grid=(faces,),
            in_specs=[
                pl.BlockSpec((1, ext_rows, ext_cols, chans), lambda f, o: (f, 0, 0, 0)),
                pl.BlockSpec((1, rows, cols, chans), lambda f, o: (f, 0, 0, 0)),
            ],
            out_specs=pl.BlockSpec((taps, 8, chans), lambda f, o: (0, 0, 0)),
            scratch_shapes=[pltpu.VMEM((BOX, block + 2 * RADIUS, cols, chans), jnp.float32)],
        ),
        out_shape=jax.ShapeDtypeStruct((taps, 8, chans), jnp.float32),
        compiler_params=pltpu.CompilerParams(
            dimension_semantics=("arbitrary",), vmem_limit_bytes=56 * 1024 * 1024
        ),
    )(offsets.reshape(-1), ext, agg_grad)
    return jnp.sum(partial, axis=1)


def with_halo(cells, sides, width):
    for axis, dim in sides:
        count = lax.axis_size(axis)
        ends = count - 1
        head = lax.slice_in_dim(cells, 0, width, axis=dim)
        tail = lax.slice_in_dim(cells, cells.shape[dim] - width, cells.shape[dim], axis=dim)
        cells = jnp.concatenate(
            [
                lax.ppermute(tail, axis, [(i, (i + 1) % count) for i in range(ends)]),
                cells,
                lax.ppermute(head, axis, [((i + 1) % count, i) for i in range(ends)]),
            ],
            axis=dim,
        )
    return cells


def cut_segment(padded_edges, face_local, side_index, flip_flag, start_cell, length):
    padded_len = padded_edges.shape[3]
    begin_cell = jnp.where(flip_flag == 1, padded_len - start_cell - length, start_cell)
    zero_index = jnp.zeros((), jnp.int32)
    segment = lax.dynamic_slice(
        padded_edges,
        (face_local, side_index, zero_index, begin_cell, zero_index),
        (1, 1, padded_edges.shape[2], length, padded_edges.shape[4]),
    )[0, 0]
    return jnp.where(flip_flag == 1, jnp.flip(segment, axis=1), segment)


def shards(state, offsets, links, stencil, gain, w_in, w_out, cotangent):
    local_count, rows_dev, cols_dev, channels = state.shape
    row_count = lax.axis_size("row")
    col_count = lax.axis_size("col")
    face_count = lax.axis_size("face")
    face_side = rows_dev * row_count
    piece_cells = face_side // (row_count * col_count)
    row_index = lax.axis_index("row")
    col_index = lax.axis_index("col")
    face_index = lax.axis_index("face")
    radius_cells = RADIUS
    extended = with_halo(state, (("row", 1), ("col", 2)), RADIUS)
    top_strip = state[:, :radius_cells]
    bottom_strip = jnp.flip(state[:, rows_dev - radius_cells :], axis=1)
    left_strip = jnp.swapaxes(state[:, :, :radius_cells], 1, 2)
    right_strip = jnp.swapaxes(jnp.flip(state[:, :, cols_dev - radius_cells :], axis=2), 1, 2)
    across = jnp.where(row_index == 0, top_strip, bottom_strip)
    downward = jnp.where(col_index == 0, left_strip, right_strip)
    sub_across = cols_dev // row_count
    sub_down = rows_dev // col_count
    across_sub = lax.all_to_all(
        across.reshape(local_count, radius_cells, row_count, sub_across, channels),
        "row",
        split_axis=2,
        concat_axis=2,
        tiled=True,
    )
    down_sub = lax.all_to_all(
        downward.reshape(local_count, radius_cells, col_count, sub_down, channels),
        "col",
        split_axis=2,
        concat_axis=2,
        tiled=True,
    )
    own_across = jnp.stack([across_sub[:, :, 0], across_sub[:, :, row_count - 1]], axis=1)
    own_down = jnp.stack([down_sub[:, :, 0], down_sub[:, :, col_count - 1]], axis=1)
    across_all = lax.all_gather(own_across, ("row", "col")).reshape(
        row_count, col_count, local_count, 2, radius_cells, sub_across, channels
    )
    down_all = lax.all_gather(own_down, ("row", "col")).reshape(
        row_count, col_count, local_count, 2, radius_cells, sub_down, channels
    )
    across_full = jnp.transpose(across_all, (2, 3, 4, 1, 0, 5, 6)).reshape(
        local_count, 2, radius_cells, face_side, channels
    )
    down_full = jnp.transpose(down_all, (2, 3, 4, 0, 1, 5, 6)).reshape(
        local_count, 2, radius_cells, face_side, channels
    )
    side_edges = jnp.concatenate([across_full, down_full], axis=1)
    across_side = jnp.where(row_index == 0, 0, 1).astype(jnp.int32)
    down_side = jnp.where(col_index == 0, 2, 3).astype(jnp.int32)
    across_len = cols_dev + 2 * radius_cells
    down_len = rows_dev + 2 * radius_cells
    edge_pad = ((0, 0), (0, 0), (0, 0), (radius_cells, radius_cells), (0, 0))
    padded_edges = jnp.pad(side_edges, edge_pad)
    across_list = []
    down_list = []
    for dest_face in range(local_count * face_count):
        link_across = lax.dynamic_index_in_dim(links[dest_face], across_side, 0, keepdims=False)
        link_down = lax.dynamic_index_in_dim(links[dest_face], down_side, 0, keepdims=False)
        segment_across = cut_segment(
            padded_edges,
            link_across[0] % local_count,
            link_across[1],
            link_across[2],
            col_index * cols_dev,
            across_len,
        )
        segment_down = cut_segment(
            padded_edges,
            link_down[0] % local_count,
            link_down[1],
            link_down[2],
            row_index * rows_dev,
            down_len,
        )
        across_list.append(
            jnp.where(
                link_across[0] // local_count == face_index,
                segment_across,
                jnp.zeros_like(segment_across),
            )
        )
        down_list.append(
            jnp.where(
                link_down[0] // local_count == face_index,
                segment_down,
                jnp.zeros_like(segment_down),
            )
        )
    got_across, got_down = (
        lax.all_to_all(jnp.stack(across_list), "face", split_axis=0, concat_axis=0, tiled=True),
        lax.all_to_all(jnp.stack(down_list), "face", split_axis=0, concat_axis=0, tiled=True),
    )
    halo_across = jnp.sum(
        got_across.reshape(face_count, local_count, radius_cells, across_len, channels), axis=0
    )
    halo_down = jnp.sum(
        got_down.reshape(face_count, local_count, radius_cells, down_len, channels), axis=0
    )
    top_part = jnp.where(row_index == 0, jnp.flip(halo_across, axis=1), jnp.zeros_like(halo_across))
    bottom_part = jnp.where(row_index == row_count - 1, halo_across, jnp.zeros_like(halo_across))
    left_block = jnp.swapaxes(jnp.flip(halo_down, axis=1), 1, 2)
    right_block = jnp.swapaxes(halo_down, 1, 2)
    left_part = jnp.where(col_index == 0, left_block, jnp.zeros_like(left_block))
    right_part = jnp.where(col_index == col_count - 1, right_block, jnp.zeros_like(right_block))
    extended = extended.at[:, :radius_cells].add(top_part)
    extended = extended.at[:, radius_cells + rows_dev :].add(bottom_part)
    extended = extended.at[:, :, :radius_cells].add(left_part)
    extended = extended.at[:, :, radius_cells + cols_dev :].add(right_part)
    box_side = 2 * radius_cells + 1
    box_index = (offsets[:, 0] + radius_cells) * box_side + offsets[:, 1] + radius_cells
    onehot = (
        box_index[:, None] == jnp.arange(box_side * box_side, dtype=jnp.int32)[None, :]
    ).astype(jnp.float32)
    box_weights = jnp.dot(onehot.T, stencil.astype(jnp.float32), precision=lax.Precision.HIGHEST)
    aggregated = stencil_forward(extended, box_weights)
    cell_count = local_count * rows_dev * cols_dev
    aggregated = aggregated.reshape(cell_count, channels)
    mean_square = jnp.mean(aggregated * aggregated, axis=-1, keepdims=True)
    inverse_rms = lax.rsqrt(mean_square + 1e-05)
    normalized = aggregated * inverse_rms
    gain_float = gain.astype(jnp.float32)
    hidden_in = (normalized * gain_float).astype(jnp.bfloat16)
    pre_act = jnp.dot(hidden_in, w_in, preferred_element_type=jnp.float32)
    sigmoid_pre = jax.nn.sigmoid(pre_act)
    activated = (pre_act * sigmoid_pre).astype(jnp.bfloat16)
    increment = jnp.dot(activated, w_out, preferred_element_type=jnp.float32).astype(jnp.bfloat16)
    target_rows = cotangent.reshape(cell_count, channels)
    contract_rows = (((0,), (0,)), ((), ()))
    contract_cols = (((1,), (1,)), ((), ()))
    w_out_grad = lax.dot_general(
        activated, target_rows, contract_rows, preferred_element_type=jnp.float32
    )
    act_grad = lax.dot_general(
        target_rows, w_out, contract_cols, preferred_element_type=jnp.float32
    )
    pre_grad = (act_grad * sigmoid_pre * (1.0 + pre_act * (1.0 - sigmoid_pre))).astype(jnp.bfloat16)
    w_in_grad = lax.dot_general(
        hidden_in, pre_grad, contract_rows, preferred_element_type=jnp.float32
    )
    hidden_grad = lax.dot_general(pre_grad, w_in, contract_cols, preferred_element_type=jnp.float32)
    gain_grad = jnp.sum(hidden_grad * normalized, axis=0)
    out_rows = w_out_grad.shape[0]
    w_in_grad, out_and_gain = lax.psum(
        (w_in_grad, jnp.concatenate([w_out_grad, gain_grad[None, :]], axis=0)),
        ("face", "row", "col"),
    )
    w_out_grad = out_and_gain[:out_rows]
    gain_grad = out_and_gain[out_rows]
    scaled_grad = hidden_grad * gain_float
    aggregated_grad = inverse_rms * (
        scaled_grad - normalized * jnp.mean(scaled_grad * normalized, axis=-1, keepdims=True)
    )
    aggregated_grad = aggregated_grad.reshape(local_count, rows_dev, cols_dev, channels)
    stencil_grad = stencil_backward(offsets, extended, aggregated_grad)
    stencil_grad, w_in_grad, out_and_gain = lax.optimization_barrier(
        (stencil_grad, w_in_grad, out_and_gain)
    )
    w_out_grad = out_and_gain[:out_rows]
    gain_grad = out_and_gain[out_rows]
    stencil_grad = butterfly_sum(stencil_grad, ("face", "row", "col"))
    return (increment.reshape(state.shape), stencil_grad, gain_grad, w_in_grad, w_out_grad)


def butterfly_sum(value, axes):
    for axis in axes:
        count = lax.axis_size(axis)
        if count & (count - 1):
            value = lax.psum(value, axis)
            continue
        step = 1
        while step < count:
            value = value + lax.ppermute(value, axis, [(i, i ^ step) for i in range(count)])
            step *= 2
    return value


def solution(mesh):
    in_specs = (
        P("face", "row", "col", None),
        P(),
        P(),
        P(),
        P(),
        P(),
        P(),
        P("face", "row", "col", None),
    )
    out_specs = (P("face", "row", "col", None), P(), P(), P(), P())
    return jax.shard_map(shards, mesh=mesh, in_specs=in_specs, out_specs=out_specs, check_vma=False)
```

```python
import jax
import jax.numpy as jnp
from jax import lax
from jax.experimental import pallas as pl
from jax.experimental.pallas import tpu as pltpu
from jax.sharding import PartitionSpec as P

RADIUS = 4
BOX = 2 * RADIUS + 1


def _fwd_kernel(ext_ref, w_ref, out_ref, shift_ref):
    rows = out_ref.shape[1]
    cols = out_ref.shape[2]
    ext_rows = ext_ref.shape[1]
    row_block = 4 if rows % 4 == 0 else 1
    for dj in range(BOX):
        def shift_row(r, carry):
            shift_ref[r] = ext_ref[0, r, pl.ds(dj, cols), :].astype(jnp.float32)
            return carry

        lax.fori_loop(0, ext_rows, shift_row, 0)
        weights = [w_ref[pl.ds(di * BOX + dj, 1), :] for di in range(BOX)]

        def out_rows(block_index, carry):
            first = block_index * row_block
            if dj == 0:
                accs = [jnp.zeros((cols, out_ref.shape[3]), jnp.float32) for _ in range(row_block)]
            else:
                accs = [out_ref[0, first + q] for q in range(row_block)]
            for t in range(BOX + row_block - 1):
                window = shift_ref[first + t]
                for q in range(row_block):
                    if 0 <= t - q < BOX:
                        accs[q] = accs[q] + weights[t - q] * window
            for q in range(row_block):
                out_ref[0, first + q] = accs[q]
            return carry

        lax.fori_loop(0, rows // row_block, out_rows, 0)


def stencil_forward(ext, box_weights):
    faces, ext_rows, ext_cols, chans = ext.shape
    rows = ext_rows - 2 * RADIUS
    cols = ext_cols - 2 * RADIUS
    return pl.pallas_call(
        _fwd_kernel,
        grid=(faces,),
        in_specs=[
            pl.BlockSpec((1, ext_rows, ext_cols, chans), lambda f: (f, 0, 0, 0)),
            pl.BlockSpec((BOX * BOX, chans), lambda f: (0, 0)),
        ],
        out_specs=pl.BlockSpec((1, rows, cols, chans), lambda f: (f, 0, 0, 0)),
        out_shape=jax.ShapeDtypeStruct((faces, rows, cols, chans), jnp.float32),
        scratch_shapes=[pltpu.VMEM((ext_rows, cols, chans), jnp.float32)],
        compiler_params=pltpu.CompilerParams(
            dimension_semantics=("arbitrary",), vmem_limit_bytes=48 * 1024 * 1024
        ),
    )(ext, box_weights)


def _fill_slabs(ext_ref, slab_ref, first_row):
    cols = slab_ref.shape[2]
    for dj in range(BOX):
        def shift_row(r, carry):
            slab_ref[dj, r] = ext_ref[0, first_row + r, pl.ds(dj, cols), :].astype(jnp.float32)
            return carry

        lax.fori_loop(0, slab_ref.shape[1], shift_row, 0)


def _bwd_kernel(off_ref, ext_ref, g_ref, out_ref, slab_ref):
    rows, cols, chans = g_ref.shape[1], g_ref.shape[2], g_ref.shape[3]
    block = slab_ref.shape[1] - 2 * RADIUS

    @pl.when(pl.program_id(0) == 0)
    def _():
        out_ref[...] = jnp.zeros_like(out_ref)

    for first_row in range(0, rows, block):
        _fill_slabs(ext_ref, slab_ref, first_row)

        def grad_row(i, carry):
            g = g_ref[0, first_row + i]
            for tap in range(out_ref.shape[0]):
                di = off_ref[2 * tap] + RADIUS
                dj = off_ref[2 * tap + 1] + RADIUS
                p = (g * slab_ref[dj, i + di]).reshape(cols // 8, 8, chans).sum(axis=0)
                out_ref[tap] = out_ref[tap] + p
            return carry

        lax.fori_loop(0, block, grad_row, 0)


def _slab_block(rows):
    block = min(rows, 32)
    while rows % block:
        block -= 1
    return block


def stencil_backward(offsets, ext, agg_grad):
    faces, ext_rows, ext_cols, chans = ext.shape
    rows = ext_rows - 2 * RADIUS
    cols = ext_cols - 2 * RADIUS
    taps = offsets.shape[0]
    block = _slab_block(rows)
    partial = pl.pallas_call(
        _bwd_kernel,
        grid_spec=pltpu.PrefetchScalarGridSpec(
            num_scalar_prefetch=1,
            grid=(faces,),
            in_specs=[
                pl.BlockSpec((1, ext_rows, ext_cols, chans), lambda f, o: (f, 0, 0, 0)),
                pl.BlockSpec((1, rows, cols, chans), lambda f, o: (f, 0, 0, 0)),
            ],
            out_specs=pl.BlockSpec((taps, 8, chans), lambda f, o: (0, 0, 0)),
            scratch_shapes=[pltpu.VMEM((BOX, block + 2 * RADIUS, cols, chans), jnp.float32)],
        ),
        out_shape=jax.ShapeDtypeStruct((taps, 8, chans), jnp.float32),
        compiler_params=pltpu.CompilerParams(
            dimension_semantics=("arbitrary",), vmem_limit_bytes=56 * 1024 * 1024
        ),
    )(offsets.reshape(-1), ext, agg_grad)
    return jnp.sum(partial, axis=1)


def with_halo(cells, sides, width):
    for axis, dim in sides:
        count = lax.axis_size(axis)
        ends = count - 1
        head = lax.slice_in_dim(cells, 0, width, axis=dim)
        tail = lax.slice_in_dim(cells, cells.shape[dim] - width, cells.shape[dim], axis=dim)
        cells = jnp.concatenate(
            [
                lax.ppermute(tail, axis, [(i, (i + 1) % count) for i in range(ends)]),
                cells,
                lax.ppermute(head, axis, [((i + 1) % count, i) for i in range(ends)]),
            ],
            axis=dim,
        )
    return cells


def cut_segment(padded_edges, face_local, side_index, flip_flag, start_cell, length):
    padded_len = padded_edges.shape[3]
    begin_cell = jnp.where(flip_flag == 1, padded_len - start_cell - length, start_cell)
    zero_index = jnp.zeros((), jnp.int32)
    segment = lax.dynamic_slice(
        padded_edges,
        (face_local, side_index, zero_index, begin_cell, zero_index),
        (1, 1, padded_edges.shape[2], length, padded_edges.shape[4]),
    )[0, 0]
    return jnp.where(flip_flag == 1, jnp.flip(segment, axis=1), segment)


def shards(state, offsets, links, stencil, gain, w_in, w_out, cotangent):
    local_count, rows_dev, cols_dev, channels = state.shape
    row_count = lax.axis_size("row")
    col_count = lax.axis_size("col")
    face_count = lax.axis_size("face")
    face_side = rows_dev * row_count
    piece_cells = face_side // (row_count * col_count)
    row_index = lax.axis_index("row")
    col_index = lax.axis_index("col")
    face_index = lax.axis_index("face")
    radius_cells = RADIUS
    intra = with_halo(state, (("row", 1), ("col", 2)), RADIUS)
    box_side = 2 * radius_cells + 1
    box_index = (offsets[:, 0] + radius_cells) * box_side + offsets[:, 1] + radius_cells
    onehot = (
        box_index[:, None] == jnp.arange(box_side * box_side, dtype=jnp.int32)[None, :]
    ).astype(jnp.float32)
    box_weights = jnp.dot(onehot.T, stencil.astype(jnp.float32), precision=lax.Precision.HIGHEST)
    top_strip = state[:, :radius_cells]
    bottom_strip = jnp.flip(state[:, rows_dev - radius_cells :], axis=1)
    left_strip = jnp.swapaxes(state[:, :, :radius_cells], 1, 2)
    right_strip = jnp.swapaxes(jnp.flip(state[:, :, cols_dev - radius_cells :], axis=2), 1, 2)
    across = jnp.where(row_index == 0, top_strip, bottom_strip)
    downward = jnp.where(col_index == 0, left_strip, right_strip)
    sub_across = cols_dev // row_count
    sub_down = rows_dev // col_count
    across_sub = lax.all_to_all(
        across.reshape(local_count, radius_cells, row_count, sub_across, channels),
        "row",
        split_axis=2,
        concat_axis=2,
        tiled=True,
    )
    down_sub = lax.all_to_all(
        downward.reshape(local_count, radius_cells, col_count, sub_down, channels),
        "col",
        split_axis=2,
        concat_axis=2,
        tiled=True,
    )
    own_across = jnp.stack([across_sub[:, :, 0], across_sub[:, :, row_count - 1]], axis=1)
    own_down = jnp.stack([down_sub[:, :, 0], down_sub[:, :, col_count - 1]], axis=1)
    own_across, own_down, intra = lax.optimization_barrier((own_across, own_down, intra))
    aggregated = stencil_forward(intra, box_weights)
    across_all = lax.all_gather(own_across, ("row", "col")).reshape(
        row_count, col_count, local_count, 2, radius_cells, sub_across, channels
    )
    down_all = lax.all_gather(own_down, ("row", "col")).reshape(
        row_count, col_count, local_count, 2, radius_cells, sub_down, channels
    )
    across_all, down_all, aggregated = lax.optimization_barrier((across_all, down_all, aggregated))
    across_full = jnp.transpose(across_all, (2, 3, 4, 1, 0, 5, 6)).reshape(
        local_count, 2, radius_cells, face_side, channels
    )
    down_full = jnp.transpose(down_all, (2, 3, 4, 0, 1, 5, 6)).reshape(
        local_count, 2, radius_cells, face_side, channels
    )
    side_edges = jnp.concatenate([across_full, down_full], axis=1)
    across_side = jnp.where(row_index == 0, 0, 1).astype(jnp.int32)
    down_side = jnp.where(col_index == 0, 2, 3).astype(jnp.int32)
    across_len = cols_dev + 2 * radius_cells
    down_len = rows_dev + 2 * radius_cells
    edge_pad = ((0, 0), (0, 0), (0, 0), (radius_cells, radius_cells), (0, 0))
    padded_edges = jnp.pad(side_edges, edge_pad)
    across_list = []
    down_list = []
    for dest_face in range(local_count * face_count):
        link_across = lax.dynamic_index_in_dim(links[dest_face], across_side, 0, keepdims=False)
        link_down = lax.dynamic_index_in_dim(links[dest_face], down_side, 0, keepdims=False)
        segment_across = cut_segment(
            padded_edges,
            link_across[0] % local_count,
            link_across[1],
            link_across[2],
            col_index * cols_dev,
            across_len,
        )
        segment_down = cut_segment(
            padded_edges,
            link_down[0] % local_count,
            link_down[1],
            link_down[2],
            row_index * rows_dev,
            down_len,
        )
        across_list.append(
            jnp.where(
                link_across[0] // local_count == face_index,
                segment_across,
                jnp.zeros_like(segment_across),
            )
        )
        down_list.append(
            jnp.where(
                link_down[0] // local_count == face_index,
                segment_down,
                jnp.zeros_like(segment_down),
            )
        )
    got_across, got_down = (
        lax.all_to_all(jnp.stack(across_list), "face", split_axis=0, concat_axis=0, tiled=True),
        lax.all_to_all(jnp.stack(down_list), "face", split_axis=0, concat_axis=0, tiled=True),
    )
    halo_across = jnp.sum(
        got_across.reshape(face_count, local_count, radius_cells, across_len, channels), axis=0
    )
    halo_down = jnp.sum(
        got_down.reshape(face_count, local_count, radius_cells, down_len, channels), axis=0
    )
    top_part = jnp.where(row_index == 0, jnp.flip(halo_across, axis=1), jnp.zeros_like(halo_across))
    bottom_part = jnp.where(row_index == row_count - 1, halo_across, jnp.zeros_like(halo_across))
    left_block = jnp.swapaxes(jnp.flip(halo_down, axis=1), 1, 2)
    right_block = jnp.swapaxes(halo_down, 1, 2)
    left_part = jnp.where(col_index == 0, left_block, jnp.zeros_like(left_block))
    right_part = jnp.where(col_index == col_count - 1, right_block, jnp.zeros_like(right_block))
    extended = intra.at[:, :radius_cells].add(top_part)
    extended = extended.at[:, radius_cells + rows_dev :].add(bottom_part)
    extended = extended.at[:, :, :radius_cells].add(left_part)
    extended = extended.at[:, :, radius_cells + cols_dev :].add(right_part)
    box_flipped = jnp.transpose(box_weights.reshape(box_side, box_side, channels), (1, 0, 2)).reshape(
        box_side * box_side, channels
    )
    pad_rows = jnp.zeros((local_count, 2 * radius_cells, across_len, channels), state.dtype)
    row_bands = jnp.concatenate(
        [
            jnp.concatenate([top_part, pad_rows], axis=1),
            jnp.concatenate([pad_rows, bottom_part], axis=1),
        ],
        axis=0,
    )
    row_fix = stencil_forward(row_bands, box_weights)
    left_rows = jnp.swapaxes(left_part, 1, 2)
    right_rows = jnp.swapaxes(right_part, 1, 2)
    pad_cols = jnp.zeros((local_count, 2 * radius_cells, down_len, channels), state.dtype)
    col_bands = jnp.concatenate(
        [
            jnp.concatenate([left_rows, pad_cols], axis=1),
            jnp.concatenate([pad_cols, right_rows], axis=1),
        ],
        axis=0,
    )
    col_fix = jnp.swapaxes(stencil_forward(col_bands, box_flipped), 1, 2)
    aggregated = aggregated.at[:, :radius_cells].add(row_fix[:local_count])
    aggregated = aggregated.at[:, rows_dev - radius_cells :].add(row_fix[local_count:])
    aggregated = aggregated.at[:, :, :radius_cells].add(col_fix[:local_count])
    aggregated = aggregated.at[:, :, cols_dev - radius_cells :].add(col_fix[local_count:])
    cell_count = local_count * rows_dev * cols_dev
    aggregated = aggregated.reshape(cell_count, channels)
    mean_square = jnp.mean(aggregated * aggregated, axis=-1, keepdims=True)
    inverse_rms = lax.rsqrt(mean_square + 1e-05)
    normalized = aggregated * inverse_rms
    gain_float = gain.astype(jnp.float32)
    hidden_in = (normalized * gain_float).astype(jnp.bfloat16)
    pre_act = jnp.dot(hidden_in, w_in, preferred_element_type=jnp.float32)
    sigmoid_pre = jax.nn.sigmoid(pre_act)
    activated = (pre_act * sigmoid_pre).astype(jnp.bfloat16)
    increment = jnp.dot(activated, w_out, preferred_element_type=jnp.float32).astype(jnp.bfloat16)
    target_rows = cotangent.reshape(cell_count, channels)
    contract_rows = (((0,), (0,)), ((), ()))
    contract_cols = (((1,), (1,)), ((), ()))
    w_out_grad = lax.dot_general(
        activated, target_rows, contract_rows, preferred_element_type=jnp.float32
    )
    act_grad = lax.dot_general(
        target_rows, w_out, contract_cols, preferred_element_type=jnp.float32
    )
    pre_grad = (act_grad * sigmoid_pre * (1.0 + pre_act * (1.0 - sigmoid_pre))).astype(jnp.bfloat16)
    w_in_grad = lax.dot_general(
        hidden_in, pre_grad, contract_rows, preferred_element_type=jnp.float32
    )
    hidden_grad = lax.dot_general(pre_grad, w_in, contract_cols, preferred_element_type=jnp.float32)
    gain_grad = jnp.sum(hidden_grad * normalized, axis=0)
    out_rows = w_out_grad.shape[0]
    w_in_grad, out_and_gain = lax.psum(
        (w_in_grad, jnp.concatenate([w_out_grad, gain_grad[None, :]], axis=0)),
        ("face", "row", "col"),
    )
    w_out_grad = out_and_gain[:out_rows]
    gain_grad = out_and_gain[out_rows]
    scaled_grad = hidden_grad * gain_float
    aggregated_grad = inverse_rms * (
        scaled_grad - normalized * jnp.mean(scaled_grad * normalized, axis=-1, keepdims=True)
    )
    aggregated_grad = aggregated_grad.reshape(local_count, rows_dev, cols_dev, channels)
    stencil_grad = stencil_backward(offsets, extended, aggregated_grad)
    stencil_grad, w_in_grad, out_and_gain = lax.optimization_barrier(
        (stencil_grad, w_in_grad, out_and_gain)
    )
    w_out_grad = out_and_gain[:out_rows]
    gain_grad = out_and_gain[out_rows]
    stencil_grad = butterfly_sum(stencil_grad, ("face", "row", "col"))
    return (increment.reshape(state.shape), stencil_grad, gain_grad, w_in_grad, w_out_grad)


def butterfly_sum(value, axes):
    for axis in axes:
        count = lax.axis_size(axis)
        if count & (count - 1):
            value = lax.psum(value, axis)
            continue
        step = 1
        while step < count:
            value = value + lax.ppermute(value, axis, [(i, i ^ step) for i in range(count)])
            step *= 2
    return value


def solution(mesh):
    in_specs = (
        P("face", "row", "col", None),
        P(),
        P(),
        P(),
        P(),
        P(),
        P(),
        P("face", "row", "col", None),
    )
    out_specs = (P("face", "row", "col", None), P(), P(), P(), P())
    return jax.shard_map(shards, mesh=mesh, in_specs=in_specs, out_specs=out_specs, check_vma=False)
```

```python
import jax
import jax.numpy as jnp
from jax import lax
from jax.experimental import pallas as pl
from jax.experimental.pallas import tpu as pltpu
from jax.sharding import PartitionSpec as P

RADIUS = 4
BOX = 2 * RADIUS + 1


def _fwd_kernel(ext_ref, w_ref, out_ref, shift_ref):
    rows = out_ref.shape[1]
    cols = out_ref.shape[2]
    ext_rows = ext_ref.shape[1]
    row_block = 4 if rows % 4 == 0 else 1
    for dj in range(BOX):
        def shift_row(r, carry):
            shift_ref[r] = ext_ref[0, r, pl.ds(dj, cols), :].astype(jnp.float32)
            return carry

        lax.fori_loop(0, ext_rows, shift_row, 0)
        weights = [w_ref[pl.ds(di * BOX + dj, 1), :] for di in range(BOX)]

        def out_rows(block_index, carry):
            first = block_index * row_block
            if dj == 0:
                accs = [jnp.zeros((cols, out_ref.shape[3]), jnp.float32) for _ in range(row_block)]
            else:
                accs = [out_ref[0, first + q] for q in range(row_block)]
            for t in range(BOX + row_block - 1):
                window = shift_ref[first + t]
                for q in range(row_block):
                    if 0 <= t - q < BOX:
                        accs[q] = accs[q] + weights[t - q] * window
            for q in range(row_block):
                out_ref[0, first + q] = accs[q]
            return carry

        lax.fori_loop(0, rows // row_block, out_rows, 0)


def stencil_forward(ext, box_weights):
    faces, ext_rows, ext_cols, chans = ext.shape
    rows = ext_rows - 2 * RADIUS
    cols = ext_cols - 2 * RADIUS
    return pl.pallas_call(
        _fwd_kernel,
        grid=(faces,),
        in_specs=[
            pl.BlockSpec((1, ext_rows, ext_cols, chans), lambda f: (f, 0, 0, 0)),
            pl.BlockSpec((BOX * BOX, chans), lambda f: (0, 0)),
        ],
        out_specs=pl.BlockSpec((1, rows, cols, chans), lambda f: (f, 0, 0, 0)),
        out_shape=jax.ShapeDtypeStruct((faces, rows, cols, chans), jnp.float32),
        scratch_shapes=[pltpu.VMEM((ext_rows, cols, chans), jnp.float32)],
        compiler_params=pltpu.CompilerParams(
            dimension_semantics=("arbitrary",), vmem_limit_bytes=48 * 1024 * 1024
        ),
    )(ext, box_weights)


def _fill_slabs(ext_ref, slab_ref, first_row):
    cols = slab_ref.shape[2]
    for dj in range(BOX):
        def shift_row(r, carry):
            slab_ref[dj, r] = ext_ref[0, first_row + r, pl.ds(dj, cols), :].astype(jnp.float32)
            return carry

        lax.fori_loop(0, slab_ref.shape[1], shift_row, 0)


def _bwd_kernel(off_ref, ext_ref, g_ref, out_ref, slab_ref):
    rows, cols, chans = g_ref.shape[1], g_ref.shape[2], g_ref.shape[3]
    block = slab_ref.shape[1] - 2 * RADIUS

    @pl.when(pl.program_id(0) == 0)
    def _():
        out_ref[...] = jnp.zeros_like(out_ref)

    for first_row in range(0, rows, block):
        _fill_slabs(ext_ref, slab_ref, first_row)

        def grad_row(i, carry):
            g = g_ref[0, first_row + i]
            for tap in range(out_ref.shape[0]):
                di = off_ref[2 * tap] + RADIUS
                dj = off_ref[2 * tap + 1] + RADIUS
                p = (g * slab_ref[dj, i + di]).reshape(cols // 8, 8, chans).sum(axis=0)
                out_ref[tap] = out_ref[tap] + p
            return carry

        lax.fori_loop(0, block, grad_row, 0)


def _slab_block(rows):
    block = min(rows, 32)
    while rows % block:
        block -= 1
    return block


def stencil_backward(offsets, ext, agg_grad):
    faces, ext_rows, ext_cols, chans = ext.shape
    rows = ext_rows - 2 * RADIUS
    cols = ext_cols - 2 * RADIUS
    taps = offsets.shape[0]
    block = _slab_block(rows)
    partial = pl.pallas_call(
        _bwd_kernel,
        grid_spec=pltpu.PrefetchScalarGridSpec(
            num_scalar_prefetch=1,
            grid=(faces,),
            in_specs=[
                pl.BlockSpec((1, ext_rows, ext_cols, chans), lambda f, o: (f, 0, 0, 0)),
                pl.BlockSpec((1, rows, cols, chans), lambda f, o: (f, 0, 0, 0)),
            ],
            out_specs=pl.BlockSpec((taps, 8, chans), lambda f, o: (0, 0, 0)),
            scratch_shapes=[pltpu.VMEM((BOX, block + 2 * RADIUS, cols, chans), jnp.float32)],
        ),
        out_shape=jax.ShapeDtypeStruct((taps, 8, chans), jnp.float32),
        compiler_params=pltpu.CompilerParams(
            dimension_semantics=("arbitrary",), vmem_limit_bytes=56 * 1024 * 1024
        ),
    )(offsets.reshape(-1), ext, agg_grad)
    return jnp.sum(partial, axis=1)


def with_halo(cells, sides, width):
    for axis, dim in sides:
        count = lax.axis_size(axis)
        ends = count - 1
        head = lax.slice_in_dim(cells, 0, width, axis=dim)
        tail = lax.slice_in_dim(cells, cells.shape[dim] - width, cells.shape[dim], axis=dim)
        cells = jnp.concatenate(
            [
                lax.ppermute(tail, axis, [(i, (i + 1) % count) for i in range(ends)]),
                cells,
                lax.ppermute(head, axis, [((i + 1) % count, i) for i in range(ends)]),
            ],
            axis=dim,
        )
    return cells


def cut_segment(padded_edges, face_local, side_index, flip_flag, start_cell, length):
    padded_len = padded_edges.shape[3]
    begin_cell = jnp.where(flip_flag == 1, padded_len - start_cell - length, start_cell)
    zero_index = jnp.zeros((), jnp.int32)
    segment = lax.dynamic_slice(
        padded_edges,
        (face_local, side_index, zero_index, begin_cell, zero_index),
        (1, 1, padded_edges.shape[2], length, padded_edges.shape[4]),
    )[0, 0]
    return jnp.where(flip_flag == 1, jnp.flip(segment, axis=1), segment)


def shards(state, offsets, links, stencil, gain, w_in, w_out, cotangent):
    local_count, rows_dev, cols_dev, channels = state.shape
    row_count = lax.axis_size("row")
    col_count = lax.axis_size("col")
    face_count = lax.axis_size("face")
    face_side = rows_dev * row_count
    piece_cells = face_side // (row_count * col_count)
    row_index = lax.axis_index("row")
    col_index = lax.axis_index("col")
    face_index = lax.axis_index("face")
    radius_cells = RADIUS
    extended = with_halo(state, (("row", 1), ("col", 2)), RADIUS)
    top_strip = state[:, :radius_cells]
    bottom_strip = jnp.flip(state[:, rows_dev - radius_cells :], axis=1)
    left_strip = jnp.swapaxes(state[:, :, :radius_cells], 1, 2)
    right_strip = jnp.swapaxes(jnp.flip(state[:, :, cols_dev - radius_cells :], axis=2), 1, 2)
    across = jnp.where(row_index == 0, top_strip, bottom_strip)
    downward = jnp.where(col_index == 0, left_strip, right_strip)
    sub_across = cols_dev // row_count
    sub_down = rows_dev // col_count
    across_sub = lax.all_to_all(
        across.reshape(local_count, radius_cells, row_count, sub_across, channels),
        "row",
        split_axis=2,
        concat_axis=2,
        tiled=True,
    )
    down_sub = lax.all_to_all(
        downward.reshape(local_count, radius_cells, col_count, sub_down, channels),
        "col",
        split_axis=2,
        concat_axis=2,
        tiled=True,
    )
    own_across = jnp.stack([across_sub[:, :, 0], across_sub[:, :, row_count - 1]], axis=1)
    own_down = jnp.stack([down_sub[:, :, 0], down_sub[:, :, col_count - 1]], axis=1)
    if own_across.shape == own_down.shape:
        both_all = lax.all_gather(jnp.concatenate([own_across, own_down], axis=1), ("row", "col"))
        across_all = both_all[:, :, :2]
        down_all = both_all[:, :, 2:]
    else:
        across_all = lax.all_gather(own_across, ("row", "col"))
        down_all = lax.all_gather(own_down, ("row", "col"))
    across_all = across_all.reshape(
        row_count, col_count, local_count, 2, radius_cells, sub_across, channels
    )
    down_all = down_all.reshape(
        row_count, col_count, local_count, 2, radius_cells, sub_down, channels
    )
    across_full = jnp.transpose(across_all, (2, 3, 4, 1, 0, 5, 6)).reshape(
        local_count, 2, radius_cells, face_side, channels
    )
    down_full = jnp.transpose(down_all, (2, 3, 4, 0, 1, 5, 6)).reshape(
        local_count, 2, radius_cells, face_side, channels
    )
    side_edges = jnp.concatenate([across_full, down_full], axis=1)
    across_side = jnp.where(row_index == 0, 0, 1).astype(jnp.int32)
    down_side = jnp.where(col_index == 0, 2, 3).astype(jnp.int32)
    across_len = cols_dev + 2 * radius_cells
    down_len = rows_dev + 2 * radius_cells
    edge_pad = ((0, 0), (0, 0), (0, 0), (radius_cells, radius_cells), (0, 0))
    padded_edges = jnp.pad(side_edges, edge_pad)
    across_list = []
    down_list = []
    for dest_face in range(local_count * face_count):
        link_across = lax.dynamic_index_in_dim(links[dest_face], across_side, 0, keepdims=False)
        link_down = lax.dynamic_index_in_dim(links[dest_face], down_side, 0, keepdims=False)
        segment_across = cut_segment(
            padded_edges,
            link_across[0] % local_count,
            link_across[1],
            link_across[2],
            col_index * cols_dev,
            across_len,
        )
        segment_down = cut_segment(
            padded_edges,
            link_down[0] % local_count,
            link_down[1],
            link_down[2],
            row_index * rows_dev,
            down_len,
        )
        across_list.append(
            jnp.where(
                link_across[0] // local_count == face_index,
                segment_across,
                jnp.zeros_like(segment_across),
            )
        )
        down_list.append(
            jnp.where(
                link_down[0] // local_count == face_index,
                segment_down,
                jnp.zeros_like(segment_down),
            )
        )
    got_across, got_down = (
        lax.all_to_all(jnp.stack(across_list), "face", split_axis=0, concat_axis=0, tiled=True),
        lax.all_to_all(jnp.stack(down_list), "face", split_axis=0, concat_axis=0, tiled=True),
    )
    halo_across = jnp.sum(
        got_across.reshape(face_count, local_count, radius_cells, across_len, channels), axis=0
    )
    halo_down = jnp.sum(
        got_down.reshape(face_count, local_count, radius_cells, down_len, channels), axis=0
    )
    top_part = jnp.where(row_index == 0, jnp.flip(halo_across, axis=1), jnp.zeros_like(halo_across))
    bottom_part = jnp.where(row_index == row_count - 1, halo_across, jnp.zeros_like(halo_across))
    left_block = jnp.swapaxes(jnp.flip(halo_down, axis=1), 1, 2)
    right_block = jnp.swapaxes(halo_down, 1, 2)
    left_part = jnp.where(col_index == 0, left_block, jnp.zeros_like(left_block))
    right_part = jnp.where(col_index == col_count - 1, right_block, jnp.zeros_like(right_block))
    extended = extended.at[:, :radius_cells].add(top_part)
    extended = extended.at[:, radius_cells + rows_dev :].add(bottom_part)
    extended = extended.at[:, :, :radius_cells].add(left_part)
    extended = extended.at[:, :, radius_cells + cols_dev :].add(right_part)
    box_side = 2 * radius_cells + 1
    box_index = (offsets[:, 0] + radius_cells) * box_side + offsets[:, 1] + radius_cells
    onehot = (
        box_index[:, None] == jnp.arange(box_side * box_side, dtype=jnp.int32)[None, :]
    ).astype(jnp.float32)
    box_weights = jnp.dot(onehot.T, stencil.astype(jnp.float32), precision=lax.Precision.HIGHEST)
    aggregated = stencil_forward(extended, box_weights)
    cell_count = local_count * rows_dev * cols_dev
    aggregated = aggregated.reshape(cell_count, channels)
    mean_square = jnp.mean(aggregated * aggregated, axis=-1, keepdims=True)
    inverse_rms = lax.rsqrt(mean_square + 1e-05)
    normalized = aggregated * inverse_rms
    gain_float = gain.astype(jnp.float32)
    hidden_in = (normalized * gain_float).astype(jnp.bfloat16)
    pre_act = jnp.dot(hidden_in, w_in, preferred_element_type=jnp.float32)
    sigmoid_pre = jax.nn.sigmoid(pre_act)
    activated = (pre_act * sigmoid_pre).astype(jnp.bfloat16)
    increment = jnp.dot(activated, w_out, preferred_element_type=jnp.float32).astype(jnp.bfloat16)
    target_rows = cotangent.reshape(cell_count, channels)
    contract_rows = (((0,), (0,)), ((), ()))
    contract_cols = (((1,), (1,)), ((), ()))
    w_out_grad = lax.dot_general(
        activated, target_rows, contract_rows, preferred_element_type=jnp.float32
    )
    act_grad = lax.dot_general(
        target_rows, w_out, contract_cols, preferred_element_type=jnp.float32
    )
    pre_grad = (act_grad * sigmoid_pre * (1.0 + pre_act * (1.0 - sigmoid_pre))).astype(jnp.bfloat16)
    w_in_grad = lax.dot_general(
        hidden_in, pre_grad, contract_rows, preferred_element_type=jnp.float32
    )
    hidden_grad = lax.dot_general(pre_grad, w_in, contract_cols, preferred_element_type=jnp.float32)
    gain_grad = jnp.sum(hidden_grad * normalized, axis=0)
    out_rows = w_out_grad.shape[0]
    w_in_grad, out_and_gain = lax.psum(
        (w_in_grad, jnp.concatenate([w_out_grad, gain_grad[None, :]], axis=0)),
        ("face", "row", "col"),
    )
    w_out_grad = out_and_gain[:out_rows]
    gain_grad = out_and_gain[out_rows]
    scaled_grad = hidden_grad * gain_float
    aggregated_grad = inverse_rms * (
        scaled_grad - normalized * jnp.mean(scaled_grad * normalized, axis=-1, keepdims=True)
    )
    aggregated_grad = aggregated_grad.reshape(local_count, rows_dev, cols_dev, channels)
    stencil_grad = stencil_backward(offsets, extended, aggregated_grad)
    stencil_grad, w_in_grad, out_and_gain = lax.optimization_barrier(
        (stencil_grad, w_in_grad, out_and_gain)
    )
    w_out_grad = out_and_gain[:out_rows]
    gain_grad = out_and_gain[out_rows]
    stencil_grad = butterfly_sum(stencil_grad, ("face", "row", "col"))
    return (increment.reshape(state.shape), stencil_grad, gain_grad, w_in_grad, w_out_grad)


def butterfly_sum(value, axes):
    for axis in axes:
        count = lax.axis_size(axis)
        if count & (count - 1):
            value = lax.psum(value, axis)
            continue
        step = 1
        while step < count:
            value = value + lax.ppermute(value, axis, [(i, i ^ step) for i in range(count)])
            step *= 2
    return value


def solution(mesh):
    in_specs = (
        P("face", "row", "col", None),
        P(),
        P(),
        P(),
        P(),
        P(),
        P(),
        P("face", "row", "col", None),
    )
    out_specs = (P("face", "row", "col", None), P(), P(), P(), P())
    return jax.shard_map(shards, mesh=mesh, in_specs=in_specs, out_specs=out_specs, check_vma=False)
```

```python
import jax
import jax.numpy as jnp
from jax import lax
from jax.experimental import pallas as pl
from jax.experimental.pallas import tpu as pltpu
from jax.sharding import PartitionSpec as P

RADIUS = 4
BOX = 2 * RADIUS + 1


def _fwd_kernel(ext_ref, w_ref, out_ref, shift_ref):
    rows = out_ref.shape[1]
    cols = out_ref.shape[2]
    ext_rows = ext_ref.shape[1]
    row_block = 4 if rows % 4 == 0 else 1
    for dj in range(BOX):
        def shift_row(r, carry):
            shift_ref[r] = ext_ref[0, r, pl.ds(dj, cols), :].astype(jnp.float32)
            return carry

        lax.fori_loop(0, ext_rows, shift_row, 0)
        weights = [w_ref[pl.ds(di * BOX + dj, 1), :] for di in range(BOX)]

        def out_rows(block_index, carry):
            first = block_index * row_block
            if dj == 0:
                accs = [jnp.zeros((cols, out_ref.shape[3]), jnp.float32) for _ in range(row_block)]
            else:
                accs = [out_ref[0, first + q] for q in range(row_block)]
            for t in range(BOX + row_block - 1):
                window = shift_ref[first + t]
                for q in range(row_block):
                    if 0 <= t - q < BOX:
                        accs[q] = accs[q] + weights[t - q] * window
            for q in range(row_block):
                out_ref[0, first + q] = accs[q]
            return carry

        lax.fori_loop(0, rows // row_block, out_rows, 0)


def stencil_forward(ext, box_weights):
    faces, ext_rows, ext_cols, chans = ext.shape
    rows = ext_rows - 2 * RADIUS
    cols = ext_cols - 2 * RADIUS
    return pl.pallas_call(
        _fwd_kernel,
        grid=(faces,),
        in_specs=[
            pl.BlockSpec((1, ext_rows, ext_cols, chans), lambda f: (f, 0, 0, 0)),
            pl.BlockSpec((BOX * BOX, chans), lambda f: (0, 0)),
        ],
        out_specs=pl.BlockSpec((1, rows, cols, chans), lambda f: (f, 0, 0, 0)),
        out_shape=jax.ShapeDtypeStruct((faces, rows, cols, chans), jnp.float32),
        scratch_shapes=[pltpu.VMEM((ext_rows, cols, chans), jnp.float32)],
        compiler_params=pltpu.CompilerParams(
            dimension_semantics=("arbitrary",), vmem_limit_bytes=48 * 1024 * 1024
        ),
    )(ext, box_weights)


def _fill_slabs(ext_ref, slab_ref, first_row):
    cols = slab_ref.shape[2]
    for dj in range(BOX):
        def shift_row(r, carry):
            slab_ref[dj, r] = ext_ref[0, first_row + r, pl.ds(dj, cols), :].astype(jnp.float32)
            return carry

        lax.fori_loop(0, slab_ref.shape[1], shift_row, 0)


def _bwd_kernel(off_ref, ext_ref, g_ref, out_ref, slab_ref):
    rows, cols, chans = g_ref.shape[1], g_ref.shape[2], g_ref.shape[3]
    block = slab_ref.shape[1] - 2 * RADIUS

    @pl.when(pl.program_id(0) == 0)
    def _():
        out_ref[...] = jnp.zeros_like(out_ref)

    for first_row in range(0, rows, block):
        _fill_slabs(ext_ref, slab_ref, first_row)

        def grad_row(i, carry):
            g = g_ref[0, first_row + i]
            for tap in range(out_ref.shape[0]):
                di = off_ref[2 * tap] + RADIUS
                dj = off_ref[2 * tap + 1] + RADIUS
                p = (g * slab_ref[dj, i + di]).reshape(cols // 8, 8, chans).sum(axis=0)
                out_ref[tap] = out_ref[tap] + p
            return carry

        lax.fori_loop(0, block, grad_row, 0)


def _slab_block(rows):
    block = min(rows, 32)
    while rows % block:
        block -= 1
    return block


def stencil_backward(offsets, ext, agg_grad):
    faces, ext_rows, ext_cols, chans = ext.shape
    rows = ext_rows - 2 * RADIUS
    cols = ext_cols - 2 * RADIUS
    taps = offsets.shape[0]
    block = _slab_block(rows)
    partial = pl.pallas_call(
        _bwd_kernel,
        grid_spec=pltpu.PrefetchScalarGridSpec(
            num_scalar_prefetch=1,
            grid=(faces,),
            in_specs=[
                pl.BlockSpec((1, ext_rows, ext_cols, chans), lambda f, o: (f, 0, 0, 0)),
                pl.BlockSpec((1, rows, cols, chans), lambda f, o: (f, 0, 0, 0)),
            ],
            out_specs=pl.BlockSpec((taps, 8, chans), lambda f, o: (0, 0, 0)),
            scratch_shapes=[pltpu.VMEM((BOX, block + 2 * RADIUS, cols, chans), jnp.float32)],
        ),
        out_shape=jax.ShapeDtypeStruct((taps, 8, chans), jnp.float32),
        compiler_params=pltpu.CompilerParams(
            dimension_semantics=("arbitrary",), vmem_limit_bytes=56 * 1024 * 1024
        ),
    )(offsets.reshape(-1), ext, agg_grad)
    return jnp.sum(partial, axis=1)


def with_halo(cells, sides, width):
    for axis, dim in sides:
        count = lax.axis_size(axis)
        ends = count - 1
        head = lax.slice_in_dim(cells, 0, width, axis=dim)
        tail = lax.slice_in_dim(cells, cells.shape[dim] - width, cells.shape[dim], axis=dim)
        cells = jnp.concatenate(
            [
                lax.ppermute(tail, axis, [(i, (i + 1) % count) for i in range(ends)]),
                cells,
                lax.ppermute(head, axis, [((i + 1) % count, i) for i in range(ends)]),
            ],
            axis=dim,
        )
    return cells


def cut_segment(padded_edges, face_local, side_index, flip_flag, start_cell, length):
    padded_len = padded_edges.shape[3]
    begin_cell = jnp.where(flip_flag == 1, padded_len - start_cell - length, start_cell)
    zero_index = jnp.zeros((), jnp.int32)
    segment = lax.dynamic_slice(
        padded_edges,
        (face_local, side_index, zero_index, begin_cell, zero_index),
        (1, 1, padded_edges.shape[2], length, padded_edges.shape[4]),
    )[0, 0]
    return jnp.where(flip_flag == 1, jnp.flip(segment, axis=1), segment)


def shards(state, offsets, links, stencil, gain, w_in, w_out, cotangent):
    local_count, rows_dev, cols_dev, channels = state.shape
    row_count = lax.axis_size("row")
    col_count = lax.axis_size("col")
    face_count = lax.axis_size("face")
    face_side = rows_dev * row_count
    piece_cells = face_side // (row_count * col_count)
    row_index = lax.axis_index("row")
    col_index = lax.axis_index("col")
    face_index = lax.axis_index("face")
    radius_cells = RADIUS
    extended = with_halo(state, (("row", 1), ("col", 2)), RADIUS)
    top_strip = state[:, :radius_cells]
    bottom_strip = jnp.flip(state[:, rows_dev - radius_cells :], axis=1)
    left_strip = jnp.swapaxes(state[:, :, :radius_cells], 1, 2)
    right_strip = jnp.swapaxes(jnp.flip(state[:, :, cols_dev - radius_cells :], axis=2), 1, 2)
    across = jnp.where(row_index == 0, top_strip, bottom_strip)
    downward = jnp.where(col_index == 0, left_strip, right_strip)
    sub_across = cols_dev // row_count
    sub_down = rows_dev // col_count
    across_sub = lax.all_to_all(
        across.reshape(local_count, radius_cells, row_count, sub_across, channels),
        "row",
        split_axis=2,
        concat_axis=2,
        tiled=True,
    )
    down_sub = lax.all_to_all(
        downward.reshape(local_count, radius_cells, col_count, sub_down, channels),
        "col",
        split_axis=2,
        concat_axis=2,
        tiled=True,
    )
    own_across = jnp.stack([across_sub[:, :, 0], across_sub[:, :, row_count - 1]], axis=1)
    own_down = jnp.stack([down_sub[:, :, 0], down_sub[:, :, col_count - 1]], axis=1)
    if own_across.shape == own_down.shape:
        both_all = lax.all_gather(jnp.concatenate([own_across, own_down], axis=1), ("row", "col"))
        across_all = both_all[:, :, :2]
        down_all = both_all[:, :, 2:]
    else:
        across_all = lax.all_gather(own_across, ("row", "col"))
        down_all = lax.all_gather(own_down, ("row", "col"))
    across_all = across_all.reshape(
        row_count, col_count, local_count, 2, radius_cells, sub_across, channels
    )
    down_all = down_all.reshape(
        row_count, col_count, local_count, 2, radius_cells, sub_down, channels
    )
    across_full = jnp.transpose(across_all, (2, 3, 4, 1, 0, 5, 6)).reshape(
        local_count, 2, radius_cells, face_side, channels
    )
    down_full = jnp.transpose(down_all, (2, 3, 4, 0, 1, 5, 6)).reshape(
        local_count, 2, radius_cells, face_side, channels
    )
    side_edges = jnp.concatenate([across_full, down_full], axis=1)
    across_side = jnp.where(row_index == 0, 0, 1).astype(jnp.int32)
    down_side = jnp.where(col_index == 0, 2, 3).astype(jnp.int32)
    across_len = cols_dev + 2 * radius_cells
    down_len = rows_dev + 2 * radius_cells
    edge_pad = ((0, 0), (0, 0), (0, 0), (radius_cells, radius_cells), (0, 0))
    padded_edges = jnp.pad(side_edges, edge_pad)
    across_list = []
    down_list = []
    for dest_face in range(local_count * face_count):
        link_across = lax.dynamic_index_in_dim(links[dest_face], across_side, 0, keepdims=False)
        link_down = lax.dynamic_index_in_dim(links[dest_face], down_side, 0, keepdims=False)
        segment_across = cut_segment(
            padded_edges,
            link_across[0] % local_count,
            link_across[1],
            link_across[2],
            col_index * cols_dev,
            across_len,
        )
        segment_down = cut_segment(
            padded_edges,
            link_down[0] % local_count,
            link_down[1],
            link_down[2],
            row_index * rows_dev,
            down_len,
        )
        across_list.append(
            jnp.where(
                link_across[0] // local_count == face_index,
                segment_across,
                jnp.zeros_like(segment_across),
            )
        )
        down_list.append(
            jnp.where(
                link_down[0] // local_count == face_index,
                segment_down,
                jnp.zeros_like(segment_down),
            )
        )
    got_across, got_down = (
        lax.all_to_all(jnp.stack(across_list), "face", split_axis=0, concat_axis=0, tiled=True),
        lax.all_to_all(jnp.stack(down_list), "face", split_axis=0, concat_axis=0, tiled=True),
    )
    halo_across = jnp.sum(
        got_across.reshape(face_count, local_count, radius_cells, across_len, channels), axis=0
    )
    halo_down = jnp.sum(
        got_down.reshape(face_count, local_count, radius_cells, down_len, channels), axis=0
    )
    top_part = jnp.where(row_index == 0, jnp.flip(halo_across, axis=1), jnp.zeros_like(halo_across))
    bottom_part = jnp.where(row_index == row_count - 1, halo_across, jnp.zeros_like(halo_across))
    left_block = jnp.swapaxes(jnp.flip(halo_down, axis=1), 1, 2)
    right_block = jnp.swapaxes(halo_down, 1, 2)
    left_part = jnp.where(col_index == 0, left_block, jnp.zeros_like(left_block))
    right_part = jnp.where(col_index == col_count - 1, right_block, jnp.zeros_like(right_block))
    extended = extended.at[:, :radius_cells].add(top_part)
    extended = extended.at[:, radius_cells + rows_dev :].add(bottom_part)
    extended = extended.at[:, :, :radius_cells].add(left_part)
    extended = extended.at[:, :, radius_cells + cols_dev :].add(right_part)
    box_side = 2 * radius_cells + 1
    box_index = (offsets[:, 0] + radius_cells) * box_side + offsets[:, 1] + radius_cells
    onehot = (
        box_index[:, None] == jnp.arange(box_side * box_side, dtype=jnp.int32)[None, :]
    ).astype(jnp.float32)
    box_weights = jnp.dot(onehot.T, stencil.astype(jnp.float32), precision=lax.Precision.HIGHEST)
    aggregated = stencil_forward(extended, box_weights)
    cell_count = local_count * rows_dev * cols_dev
    aggregated = aggregated.reshape(cell_count, channels)
    mean_square = jnp.mean(aggregated * aggregated, axis=-1, keepdims=True)
    inverse_rms = lax.rsqrt(mean_square + 1e-05)
    normalized = aggregated * inverse_rms
    gain_float = gain.astype(jnp.float32)
    hidden_in = (normalized * gain_float).astype(jnp.bfloat16)
    pre_act = jnp.dot(hidden_in, w_in, preferred_element_type=jnp.float32)
    sigmoid_pre = jax.nn.sigmoid(pre_act)
    activated = (pre_act * sigmoid_pre).astype(jnp.bfloat16)
    increment = jnp.dot(activated, w_out, preferred_element_type=jnp.float32).astype(jnp.bfloat16)
    target_rows = cotangent.reshape(cell_count, channels)
    contract_rows = (((0,), (0,)), ((), ()))
    contract_cols = (((1,), (1,)), ((), ()))
    w_out_grad = lax.dot_general(
        activated, target_rows, contract_rows, preferred_element_type=jnp.float32
    )
    act_grad = lax.dot_general(
        target_rows, w_out, contract_cols, preferred_element_type=jnp.float32
    )
    pre_grad = (act_grad * sigmoid_pre * (1.0 + pre_act * (1.0 - sigmoid_pre))).astype(jnp.bfloat16)
    w_in_grad = lax.dot_general(
        hidden_in, pre_grad, contract_rows, preferred_element_type=jnp.float32
    )
    w_in_grad, w_out_grad, pre_grad = lax.optimization_barrier((w_in_grad, w_out_grad, pre_grad))
    hidden_grad = lax.dot_general(pre_grad, w_in, contract_cols, preferred_element_type=jnp.float32)
    gain_grad = jnp.sum(hidden_grad * normalized, axis=0)
    w_in_grad, w_out_grad = lax.psum((w_in_grad, w_out_grad), ("face", "row", "col"))
    scaled_grad = hidden_grad * gain_float
    aggregated_grad = inverse_rms * (
        scaled_grad - normalized * jnp.mean(scaled_grad * normalized, axis=-1, keepdims=True)
    )
    aggregated_grad = aggregated_grad.reshape(local_count, rows_dev, cols_dev, channels)
    stencil_grad = stencil_backward(offsets, extended, aggregated_grad)
    tap_count = stencil_grad.shape[0]
    small_grads = jnp.concatenate([stencil_grad, gain_grad[None, :]], axis=0)
    small_grads, w_in_grad, w_out_grad, increment = lax.optimization_barrier(
        (small_grads, w_in_grad, w_out_grad, increment)
    )
    small_grads = butterfly_sum(small_grads, ("face", "row", "col"))
    stencil_grad = small_grads[:tap_count]
    gain_grad = small_grads[tap_count]
    return (increment.reshape(state.shape), stencil_grad, gain_grad, w_in_grad, w_out_grad)


def butterfly_sum(value, axes):
    for axis in axes:
        count = lax.axis_size(axis)
        if count & (count - 1):
            value = lax.psum(value, axis)
            continue
        step = 1
        while step < count:
            value = value + lax.ppermute(value, axis, [(i, i ^ step) for i in range(count)])
            step *= 2
    return value


def solution(mesh):
    in_specs = (
        P("face", "row", "col", None),
        P(),
        P(),
        P(),
        P(),
        P(),
        P(),
        P("face", "row", "col", None),
    )
    out_specs = (P("face", "row", "col", None), P(), P(), P(), P())
    return jax.shard_map(shards, mesh=mesh, in_specs=in_specs, out_specs=out_specs, check_vma=False)
```

```python
import jax
import jax.numpy as jnp
from jax import lax
from jax.experimental import pallas as pl
from jax.experimental.pallas import tpu as pltpu
from jax.sharding import PartitionSpec as P

RADIUS = 4
BOX = 2 * RADIUS + 1


def _fwd_kernel(ext_ref, w_ref, out_ref, shift_ref):
    rows = out_ref.shape[1]
    cols = out_ref.shape[2]
    ext_rows = ext_ref.shape[1]
    row_block = 4 if rows % 4 == 0 else 1
    for dj in range(BOX):
        def shift_row(r, carry):
            shift_ref[r] = ext_ref[0, r, pl.ds(dj, cols), :].astype(jnp.float32)
            return carry

        lax.fori_loop(0, ext_rows, shift_row, 0)
        weights = [w_ref[pl.ds(di * BOX + dj, 1), :] for di in range(BOX)]

        def out_rows(block_index, carry):
            first = block_index * row_block
            if dj == 0:
                accs = [jnp.zeros((cols, out_ref.shape[3]), jnp.float32) for _ in range(row_block)]
            else:
                accs = [out_ref[0, first + q] for q in range(row_block)]
            for t in range(BOX + row_block - 1):
                window = shift_ref[first + t]
                for q in range(row_block):
                    if 0 <= t - q < BOX:
                        accs[q] = accs[q] + weights[t - q] * window
            for q in range(row_block):
                out_ref[0, first + q] = accs[q]
            return carry

        lax.fori_loop(0, rows // row_block, out_rows, 0)


def stencil_forward(ext, box_weights):
    faces, ext_rows, ext_cols, chans = ext.shape
    rows = ext_rows - 2 * RADIUS
    cols = ext_cols - 2 * RADIUS
    return pl.pallas_call(
        _fwd_kernel,
        grid=(faces,),
        in_specs=[
            pl.BlockSpec((1, ext_rows, ext_cols, chans), lambda f: (f, 0, 0, 0)),
            pl.BlockSpec((BOX * BOX, chans), lambda f: (0, 0)),
        ],
        out_specs=pl.BlockSpec((1, rows, cols, chans), lambda f: (f, 0, 0, 0)),
        out_shape=jax.ShapeDtypeStruct((faces, rows, cols, chans), jnp.float32),
        scratch_shapes=[pltpu.VMEM((ext_rows, cols, chans), jnp.float32)],
        compiler_params=pltpu.CompilerParams(
            dimension_semantics=("arbitrary",), vmem_limit_bytes=48 * 1024 * 1024
        ),
    )(ext, box_weights)


def _fill_slabs(ext_ref, slab_ref, first_row):
    cols = slab_ref.shape[2]
    for dj in range(BOX):
        def shift_row(r, carry):
            slab_ref[dj, r] = ext_ref[0, first_row + r, pl.ds(dj, cols), :].astype(jnp.float32)
            return carry

        lax.fori_loop(0, slab_ref.shape[1], shift_row, 0)


def _bwd_kernel(off_ref, ext_ref, g_ref, out_ref, slab_ref):
    rows, cols, chans = g_ref.shape[1], g_ref.shape[2], g_ref.shape[3]
    block = slab_ref.shape[1] - 2 * RADIUS

    @pl.when(pl.program_id(0) == 0)
    def _():
        out_ref[...] = jnp.zeros_like(out_ref)

    for first_row in range(0, rows, block):
        _fill_slabs(ext_ref, slab_ref, first_row)

        def grad_row(i, carry):
            g = g_ref[0, first_row + i]
            for tap in range(out_ref.shape[0]):
                di = off_ref[2 * tap] + RADIUS
                dj = off_ref[2 * tap + 1] + RADIUS
                p = (g * slab_ref[dj, i + di]).reshape(cols // 8, 8, chans).sum(axis=0)
                out_ref[tap] = out_ref[tap] + p
            return carry

        lax.fori_loop(0, block, grad_row, 0)


def _slab_block(rows):
    block = min(rows, 32)
    while rows % block:
        block -= 1
    return block


def stencil_backward(offsets, ext, agg_grad):
    faces, ext_rows, ext_cols, chans = ext.shape
    rows = ext_rows - 2 * RADIUS
    cols = ext_cols - 2 * RADIUS
    taps = offsets.shape[0]
    block = _slab_block(rows)
    partial = pl.pallas_call(
        _bwd_kernel,
        grid_spec=pltpu.PrefetchScalarGridSpec(
            num_scalar_prefetch=1,
            grid=(faces,),
            in_specs=[
                pl.BlockSpec((1, ext_rows, ext_cols, chans), lambda f, o: (f, 0, 0, 0)),
                pl.BlockSpec((1, rows, cols, chans), lambda f, o: (f, 0, 0, 0)),
            ],
            out_specs=pl.BlockSpec((taps, 8, chans), lambda f, o: (0, 0, 0)),
            scratch_shapes=[pltpu.VMEM((BOX, block + 2 * RADIUS, cols, chans), jnp.float32)],
        ),
        out_shape=jax.ShapeDtypeStruct((taps, 8, chans), jnp.float32),
        compiler_params=pltpu.CompilerParams(
            dimension_semantics=("arbitrary",), vmem_limit_bytes=56 * 1024 * 1024
        ),
    )(offsets.reshape(-1), ext, agg_grad)
    return jnp.sum(partial, axis=1)


def with_halo(cells, sides, width):
    for axis, dim in sides:
        count = lax.axis_size(axis)
        ends = count - 1
        head = lax.slice_in_dim(cells, 0, width, axis=dim)
        tail = lax.slice_in_dim(cells, cells.shape[dim] - width, cells.shape[dim], axis=dim)
        cells = jnp.concatenate(
            [
                lax.ppermute(tail, axis, [(i, (i + 1) % count) for i in range(ends)]),
                cells,
                lax.ppermute(head, axis, [((i + 1) % count, i) for i in range(ends)]),
            ],
            axis=dim,
        )
    return cells


def cut_segment(both_edges, face_local, side_index, flip_flag, start_cell, length):
    side_count = both_edges.shape[1] // 2
    zero_index = jnp.zeros((), jnp.int32)
    return lax.dynamic_slice(
        both_edges,
        (face_local, side_index + side_count * flip_flag, zero_index, start_cell, zero_index),
        (1, 1, both_edges.shape[2], length, both_edges.shape[4]),
    )[0, 0]


def shards(state, offsets, links, stencil, gain, w_in, w_out, cotangent):
    local_count, rows_dev, cols_dev, channels = state.shape
    row_count = lax.axis_size("row")
    col_count = lax.axis_size("col")
    face_count = lax.axis_size("face")
    face_side = rows_dev * row_count
    piece_cells = face_side // (row_count * col_count)
    row_index = lax.axis_index("row")
    col_index = lax.axis_index("col")
    face_index = lax.axis_index("face")
    radius_cells = RADIUS
    extended = with_halo(state, (("row", 1), ("col", 2)), RADIUS)
    top_strip = state[:, :radius_cells]
    bottom_strip = jnp.flip(state[:, rows_dev - radius_cells :], axis=1)
    left_strip = jnp.swapaxes(state[:, :, :radius_cells], 1, 2)
    right_strip = jnp.swapaxes(jnp.flip(state[:, :, cols_dev - radius_cells :], axis=2), 1, 2)
    across = jnp.where(row_index == 0, top_strip, bottom_strip)
    downward = jnp.where(col_index == 0, left_strip, right_strip)
    sub_across = cols_dev // row_count
    sub_down = rows_dev // col_count
    across_sub = lax.all_to_all(
        across.reshape(local_count, radius_cells, row_count, sub_across, channels),
        "row",
        split_axis=2,
        concat_axis=2,
        tiled=True,
    )
    down_sub = lax.all_to_all(
        downward.reshape(local_count, radius_cells, col_count, sub_down, channels),
        "col",
        split_axis=2,
        concat_axis=2,
        tiled=True,
    )
    own_across = jnp.stack([across_sub[:, :, 0], across_sub[:, :, row_count - 1]], axis=1)
    own_down = jnp.stack([down_sub[:, :, 0], down_sub[:, :, col_count - 1]], axis=1)
    if own_across.shape == own_down.shape:
        both_all = lax.all_gather(jnp.concatenate([own_across, own_down], axis=1), ("row", "col"))
        across_all = both_all[:, :, :2]
        down_all = both_all[:, :, 2:]
    else:
        across_all = lax.all_gather(own_across, ("row", "col"))
        down_all = lax.all_gather(own_down, ("row", "col"))
    across_all = across_all.reshape(
        row_count, col_count, local_count, 2, radius_cells, sub_across, channels
    )
    down_all = down_all.reshape(
        row_count, col_count, local_count, 2, radius_cells, sub_down, channels
    )
    across_full = jnp.transpose(across_all, (2, 3, 4, 1, 0, 5, 6)).reshape(
        local_count, 2, radius_cells, face_side, channels
    )
    down_full = jnp.transpose(down_all, (2, 3, 4, 0, 1, 5, 6)).reshape(
        local_count, 2, radius_cells, face_side, channels
    )
    side_edges = jnp.concatenate([across_full, down_full], axis=1)
    across_side = jnp.where(row_index == 0, 0, 1).astype(jnp.int32)
    down_side = jnp.where(col_index == 0, 2, 3).astype(jnp.int32)
    across_len = cols_dev + 2 * radius_cells
    down_len = rows_dev + 2 * radius_cells
    edge_pad = ((0, 0), (0, 0), (0, 0), (radius_cells, radius_cells), (0, 0))
    padded_edges = jnp.pad(side_edges, edge_pad)
    padded_edges = jnp.concatenate([padded_edges, jnp.flip(padded_edges, axis=3)], axis=1)
    across_list = []
    down_list = []
    for dest_face in range(local_count * face_count):
        link_across = lax.dynamic_index_in_dim(links[dest_face], across_side, 0, keepdims=False)
        link_down = lax.dynamic_index_in_dim(links[dest_face], down_side, 0, keepdims=False)
        segment_across = cut_segment(
            padded_edges,
            link_across[0] % local_count,
            link_across[1],
            link_across[2],
            col_index * cols_dev,
            across_len,
        )
        segment_down = cut_segment(
            padded_edges,
            link_down[0] % local_count,
            link_down[1],
            link_down[2],
            row_index * rows_dev,
            down_len,
        )
        across_list.append(
            jnp.where(
                link_across[0] // local_count == face_index,
                segment_across,
                jnp.zeros_like(segment_across),
            )
        )
        down_list.append(
            jnp.where(
                link_down[0] // local_count == face_index,
                segment_down,
                jnp.zeros_like(segment_down),
            )
        )
    got_across, got_down = (
        lax.all_to_all(jnp.stack(across_list), "face", split_axis=0, concat_axis=0, tiled=True),
        lax.all_to_all(jnp.stack(down_list), "face", split_axis=0, concat_axis=0, tiled=True),
    )
    halo_across = jnp.sum(
        got_across.reshape(face_count, local_count, radius_cells, across_len, channels), axis=0
    )
    halo_down = jnp.sum(
        got_down.reshape(face_count, local_count, radius_cells, down_len, channels), axis=0
    )
    top_part = jnp.where(row_index == 0, jnp.flip(halo_across, axis=1), jnp.zeros_like(halo_across))
    bottom_part = jnp.where(row_index == row_count - 1, halo_across, jnp.zeros_like(halo_across))
    left_block = jnp.swapaxes(jnp.flip(halo_down, axis=1), 1, 2)
    right_block = jnp.swapaxes(halo_down, 1, 2)
    left_part = jnp.where(col_index == 0, left_block, jnp.zeros_like(left_block))
    right_part = jnp.where(col_index == col_count - 1, right_block, jnp.zeros_like(right_block))
    extended = extended.at[:, :radius_cells].add(top_part)
    extended = extended.at[:, radius_cells + rows_dev :].add(bottom_part)
    extended = extended.at[:, :, :radius_cells].add(left_part)
    extended = extended.at[:, :, radius_cells + cols_dev :].add(right_part)
    box_side = 2 * radius_cells + 1
    box_index = (offsets[:, 0] + radius_cells) * box_side + offsets[:, 1] + radius_cells
    onehot = (
        box_index[:, None] == jnp.arange(box_side * box_side, dtype=jnp.int32)[None, :]
    ).astype(jnp.float32)
    box_weights = jnp.dot(onehot.T, stencil.astype(jnp.float32), precision=lax.Precision.HIGHEST)
    aggregated = stencil_forward(extended, box_weights)
    cell_count = local_count * rows_dev * cols_dev
    aggregated = aggregated.reshape(cell_count, channels)
    mean_square = jnp.mean(aggregated * aggregated, axis=-1, keepdims=True)
    inverse_rms = lax.rsqrt(mean_square + 1e-05)
    normalized = aggregated * inverse_rms
    gain_float = gain.astype(jnp.float32)
    hidden_in = (normalized * gain_float).astype(jnp.bfloat16)
    pre_act = jnp.dot(hidden_in, w_in, preferred_element_type=jnp.float32)
    sigmoid_pre = jax.nn.sigmoid(pre_act)
    activated = (pre_act * sigmoid_pre).astype(jnp.bfloat16)
    increment = jnp.dot(activated, w_out, preferred_element_type=jnp.float32).astype(jnp.bfloat16)
    target_rows = cotangent.reshape(cell_count, channels)
    contract_rows = (((0,), (0,)), ((), ()))
    contract_cols = (((1,), (1,)), ((), ()))
    w_out_grad = lax.dot_general(
        activated, target_rows, contract_rows, preferred_element_type=jnp.float32
    )
    act_grad = lax.dot_general(
        target_rows, w_out, contract_cols, preferred_element_type=jnp.float32
    )
    pre_grad = (act_grad * sigmoid_pre * (1.0 + pre_act * (1.0 - sigmoid_pre))).astype(jnp.bfloat16)
    w_in_grad = lax.dot_general(
        hidden_in, pre_grad, contract_rows, preferred_element_type=jnp.float32
    )
    w_in_grad, w_out_grad, pre_grad = lax.optimization_barrier((w_in_grad, w_out_grad, pre_grad))
    hidden_grad = lax.dot_general(pre_grad, w_in, contract_cols, preferred_element_type=jnp.float32)
    gain_grad = jnp.sum(hidden_grad * normalized, axis=0)
    w_in_grad, w_out_grad = lax.psum((w_in_grad, w_out_grad), ("face", "row", "col"))
    scaled_grad = hidden_grad * gain_float
    aggregated_grad = inverse_rms * (
        scaled_grad - normalized * jnp.mean(scaled_grad * normalized, axis=-1, keepdims=True)
    )
    aggregated_grad = aggregated_grad.reshape(local_count, rows_dev, cols_dev, channels)
    stencil_grad = stencil_backward(offsets, extended, aggregated_grad)
    tap_count = stencil_grad.shape[0]
    small_grads = jnp.concatenate([stencil_grad, gain_grad[None, :]], axis=0)
    small_grads, w_in_grad, w_out_grad, increment = lax.optimization_barrier(
        (small_grads, w_in_grad, w_out_grad, increment)
    )
    small_grads = butterfly_sum(small_grads, ("face", "row", "col"))
    stencil_grad = small_grads[:tap_count]
    gain_grad = small_grads[tap_count]
    return (increment.reshape(state.shape), stencil_grad, gain_grad, w_in_grad, w_out_grad)


def butterfly_sum(value, axes):
    for axis in axes:
        count = lax.axis_size(axis)
        if count & (count - 1):
            value = lax.psum(value, axis)
            continue
        step = 1
        while step < count:
            value = value + lax.ppermute(value, axis, [(i, i ^ step) for i in range(count)])
            step *= 2
    return value


def solution(mesh):
    in_specs = (
        P("face", "row", "col", None),
        P(),
        P(),
        P(),
        P(),
        P(),
        P(),
        P("face", "row", "col", None),
    )
    out_specs = (P("face", "row", "col", None), P(), P(), P(), P())
    return jax.shard_map(shards, mesh=mesh, in_specs=in_specs, out_specs=out_specs, check_vma=False)
```

```python
import jax
import jax.numpy as jnp
from jax import lax
from jax.experimental import pallas as pl
from jax.experimental.pallas import tpu as pltpu
from jax.sharding import PartitionSpec as P

RADIUS = 4
BOX = 2 * RADIUS + 1


def _fwd_kernel(ext_ref, w_ref, out_ref, shift_ref):
    rows = out_ref.shape[1]
    cols = out_ref.shape[2]
    ext_rows = ext_ref.shape[1]
    row_block = 4 if rows % 4 == 0 else 1
    for dj in range(BOX):
        def shift_row(r, carry):
            shift_ref[r] = ext_ref[0, r, pl.ds(dj, cols), :].astype(jnp.float32)
            return carry

        lax.fori_loop(0, ext_rows, shift_row, 0)
        weights = [w_ref[pl.ds(di * BOX + dj, 1), :] for di in range(BOX)]

        def out_rows(block_index, carry):
            first = block_index * row_block
            if dj == 0:
                accs = [jnp.zeros((cols, out_ref.shape[3]), jnp.float32) for _ in range(row_block)]
            else:
                accs = [out_ref[0, first + q] for q in range(row_block)]
            for t in range(BOX + row_block - 1):
                window = shift_ref[first + t]
                for q in range(row_block):
                    if 0 <= t - q < BOX:
                        accs[q] = accs[q] + weights[t - q] * window
            for q in range(row_block):
                out_ref[0, first + q] = accs[q]
            return carry

        lax.fori_loop(0, rows // row_block, out_rows, 0)


def stencil_forward(ext, box_weights):
    faces, ext_rows, ext_cols, chans = ext.shape
    rows = ext_rows - 2 * RADIUS
    cols = ext_cols - 2 * RADIUS
    return pl.pallas_call(
        _fwd_kernel,
        grid=(faces,),
        in_specs=[
            pl.BlockSpec((1, ext_rows, ext_cols, chans), lambda f: (f, 0, 0, 0)),
            pl.BlockSpec((BOX * BOX, chans), lambda f: (0, 0)),
        ],
        out_specs=pl.BlockSpec((1, rows, cols, chans), lambda f: (f, 0, 0, 0)),
        out_shape=jax.ShapeDtypeStruct((faces, rows, cols, chans), jnp.float32),
        scratch_shapes=[pltpu.VMEM((ext_rows, cols, chans), jnp.float32)],
        compiler_params=pltpu.CompilerParams(
            dimension_semantics=("arbitrary",), vmem_limit_bytes=48 * 1024 * 1024
        ),
    )(ext, box_weights)


def _fill_slabs(ext_ref, slab_ref, first_row):
    cols = slab_ref.shape[2]
    for dj in range(BOX):
        def shift_row(r, carry):
            slab_ref[dj, r] = ext_ref[0, first_row + r, pl.ds(dj, cols), :].astype(jnp.float32)
            return carry

        lax.fori_loop(0, slab_ref.shape[1], shift_row, 0)


def _bwd_kernel(off_ref, ext_ref, g_ref, out_ref, slab_ref):
    rows, cols, chans = g_ref.shape[1], g_ref.shape[2], g_ref.shape[3]
    block = slab_ref.shape[1] - 2 * RADIUS

    @pl.when(pl.program_id(0) == 0)
    def _():
        out_ref[...] = jnp.zeros_like(out_ref)

    for first_row in range(0, rows, block):
        _fill_slabs(ext_ref, slab_ref, first_row)

        def grad_row(i, carry):
            g = g_ref[0, first_row + i]
            for tap in range(out_ref.shape[0]):
                di = off_ref[2 * tap] + RADIUS
                dj = off_ref[2 * tap + 1] + RADIUS
                p = (g * slab_ref[dj, i + di]).reshape(cols // 8, 8, chans).sum(axis=0)
                out_ref[tap] = out_ref[tap] + p
            return carry

        lax.fori_loop(0, block, grad_row, 0)


def _slab_block(rows):
    block = min(rows, 32)
    while rows % block:
        block -= 1
    return block


def stencil_backward(offsets, ext, agg_grad):
    faces, ext_rows, ext_cols, chans = ext.shape
    rows = ext_rows - 2 * RADIUS
    cols = ext_cols - 2 * RADIUS
    taps = offsets.shape[0]
    block = _slab_block(rows)
    partial = pl.pallas_call(
        _bwd_kernel,
        grid_spec=pltpu.PrefetchScalarGridSpec(
            num_scalar_prefetch=1,
            grid=(faces,),
            in_specs=[
                pl.BlockSpec((1, ext_rows, ext_cols, chans), lambda f, o: (f, 0, 0, 0)),
                pl.BlockSpec((1, rows, cols, chans), lambda f, o: (f, 0, 0, 0)),
            ],
            out_specs=pl.BlockSpec((taps, 8, chans), lambda f, o: (0, 0, 0)),
            scratch_shapes=[pltpu.VMEM((BOX, block + 2 * RADIUS, cols, chans), jnp.float32)],
        ),
        out_shape=jax.ShapeDtypeStruct((taps, 8, chans), jnp.float32),
        compiler_params=pltpu.CompilerParams(
            dimension_semantics=("arbitrary",), vmem_limit_bytes=56 * 1024 * 1024
        ),
    )(offsets.reshape(-1), ext, agg_grad)
    return jnp.sum(partial, axis=1)


def with_halo(cells, sides, width):
    for axis, dim in sides:
        count = lax.axis_size(axis)
        ends = count - 1
        head = lax.slice_in_dim(cells, 0, width, axis=dim)
        tail = lax.slice_in_dim(cells, cells.shape[dim] - width, cells.shape[dim], axis=dim)
        cells = jnp.concatenate(
            [
                lax.ppermute(tail, axis, [(i, (i + 1) % count) for i in range(ends)]),
                cells,
                lax.ppermute(head, axis, [((i + 1) % count, i) for i in range(ends)]),
            ],
            axis=dim,
        )
    return cells


def cut_segment(padded_edges, face_local, side_index, flip_flag, start_cell, length):
    padded_len = padded_edges.shape[3]
    begin_cell = jnp.where(flip_flag == 1, padded_len - start_cell - length, start_cell)
    zero_index = jnp.zeros((), jnp.int32)
    segment = lax.dynamic_slice(
        padded_edges,
        (face_local, side_index, zero_index, begin_cell, zero_index),
        (1, 1, padded_edges.shape[2], length, padded_edges.shape[4]),
    )[0, 0]
    return jnp.where(flip_flag == 1, jnp.flip(segment, axis=1), segment)


def shards(state, offsets, links, stencil, gain, w_in, w_out, cotangent):
    local_count, rows_dev, cols_dev, channels = state.shape
    row_count = lax.axis_size("row")
    col_count = lax.axis_size("col")
    face_count = lax.axis_size("face")
    face_side = rows_dev * row_count
    piece_cells = face_side // (row_count * col_count)
    row_index = lax.axis_index("row")
    col_index = lax.axis_index("col")
    face_index = lax.axis_index("face")
    radius_cells = RADIUS
    extended = with_halo(state, (("row", 1), ("col", 2)), RADIUS)
    top_strip = state[:, :radius_cells]
    bottom_strip = jnp.flip(state[:, rows_dev - radius_cells :], axis=1)
    left_strip = jnp.swapaxes(state[:, :, :radius_cells], 1, 2)
    right_strip = jnp.swapaxes(jnp.flip(state[:, :, cols_dev - radius_cells :], axis=2), 1, 2)
    across = jnp.where(row_index == 0, top_strip, bottom_strip)
    downward = jnp.where(col_index == 0, left_strip, right_strip)
    sub_across = cols_dev // row_count
    sub_down = rows_dev // col_count
    across_sub = lax.all_to_all(
        across.reshape(local_count, radius_cells, row_count, sub_across, channels),
        "row",
        split_axis=2,
        concat_axis=2,
        tiled=True,
    )
    down_sub = lax.all_to_all(
        downward.reshape(local_count, radius_cells, col_count, sub_down, channels),
        "col",
        split_axis=2,
        concat_axis=2,
        tiled=True,
    )
    own_across = jnp.stack([across_sub[:, :, 0], across_sub[:, :, row_count - 1]], axis=1)
    own_down = jnp.stack([down_sub[:, :, 0], down_sub[:, :, col_count - 1]], axis=1)
    if own_across.shape == own_down.shape:
        both_all = lax.all_gather(jnp.concatenate([own_across, own_down], axis=1), ("row", "col"))
        across_all = both_all[:, :, :2]
        down_all = both_all[:, :, 2:]
    else:
        across_all = lax.all_gather(own_across, ("row", "col"))
        down_all = lax.all_gather(own_down, ("row", "col"))
    across_all = across_all.reshape(
        row_count, col_count, local_count, 2, radius_cells, sub_across, channels
    )
    down_all = down_all.reshape(
        row_count, col_count, local_count, 2, radius_cells, sub_down, channels
    )
    across_full = jnp.transpose(across_all, (2, 3, 4, 1, 0, 5, 6)).reshape(
        local_count, 2, radius_cells, face_side, channels
    )
    down_full = jnp.transpose(down_all, (2, 3, 4, 0, 1, 5, 6)).reshape(
        local_count, 2, radius_cells, face_side, channels
    )
    side_edges = jnp.concatenate([across_full, down_full], axis=1)
    across_side = jnp.where(row_index == 0, 0, 1).astype(jnp.int32)
    down_side = jnp.where(col_index == 0, 2, 3).astype(jnp.int32)
    across_len = cols_dev + 2 * radius_cells
    down_len = rows_dev + 2 * radius_cells
    edge_pad = ((0, 0), (0, 0), (0, 0), (radius_cells, radius_cells), (0, 0))
    padded_edges = jnp.pad(side_edges, edge_pad)
    across_list = []
    down_list = []
    for dest_face in range(local_count * face_count):
        link_across = lax.dynamic_index_in_dim(links[dest_face], across_side, 0, keepdims=False)
        link_down = lax.dynamic_index_in_dim(links[dest_face], down_side, 0, keepdims=False)
        segment_across = cut_segment(
            padded_edges,
            link_across[0] % local_count,
            link_across[1],
            link_across[2],
            col_index * cols_dev,
            across_len,
        )
        segment_down = cut_segment(
            padded_edges,
            link_down[0] % local_count,
            link_down[1],
            link_down[2],
            row_index * rows_dev,
            down_len,
        )
        across_list.append(
            jnp.where(
                link_across[0] // local_count == face_index,
                segment_across,
                jnp.zeros_like(segment_across),
            )
        )
        down_list.append(
            jnp.where(
                link_down[0] // local_count == face_index,
                segment_down,
                jnp.zeros_like(segment_down),
            )
        )
    got_across, got_down = (
        lax.all_to_all(jnp.stack(across_list), "face", split_axis=0, concat_axis=0, tiled=True),
        lax.all_to_all(jnp.stack(down_list), "face", split_axis=0, concat_axis=0, tiled=True),
    )
    halo_across = jnp.sum(
        got_across.reshape(face_count, local_count, radius_cells, across_len, channels), axis=0
    )
    halo_down = jnp.sum(
        got_down.reshape(face_count, local_count, radius_cells, down_len, channels), axis=0
    )
    top_part = jnp.where(row_index == 0, jnp.flip(halo_across, axis=1), jnp.zeros_like(halo_across))
    bottom_part = jnp.where(row_index == row_count - 1, halo_across, jnp.zeros_like(halo_across))
    left_block = jnp.swapaxes(jnp.flip(halo_down, axis=1), 1, 2)
    right_block = jnp.swapaxes(halo_down, 1, 2)
    left_part = jnp.where(col_index == 0, left_block, jnp.zeros_like(left_block))
    right_part = jnp.where(col_index == col_count - 1, right_block, jnp.zeros_like(right_block))
    extended = extended.at[:, :radius_cells].add(top_part)
    extended = extended.at[:, radius_cells + rows_dev :].add(bottom_part)
    extended = extended.at[:, :, :radius_cells].add(left_part)
    extended = extended.at[:, :, radius_cells + cols_dev :].add(right_part)
    box_side = 2 * radius_cells + 1
    box_index = (offsets[:, 0] + radius_cells) * box_side + offsets[:, 1] + radius_cells
    onehot = (
        box_index[:, None] == jnp.arange(box_side * box_side, dtype=jnp.int32)[None, :]
    ).astype(jnp.float32)
    box_weights = jnp.dot(onehot.T, stencil.astype(jnp.float32), precision=lax.Precision.HIGHEST)
    aggregated = stencil_forward(extended, box_weights)
    cell_count = local_count * rows_dev * cols_dev
    aggregated = aggregated.reshape(cell_count, channels)
    mean_square = jnp.mean(aggregated * aggregated, axis=-1, keepdims=True)
    inverse_rms = lax.rsqrt(mean_square + 1e-05)
    normalized = aggregated * inverse_rms
    gain_float = gain.astype(jnp.float32)
    hidden_in = (normalized * gain_float).astype(jnp.bfloat16)
    pre_act = jnp.dot(hidden_in, w_in, preferred_element_type=jnp.float32)
    sigmoid_pre = jax.nn.sigmoid(pre_act)
    activated = (pre_act * sigmoid_pre).astype(jnp.bfloat16)
    increment = jnp.dot(activated, w_out, preferred_element_type=jnp.float32).astype(jnp.bfloat16)
    target_rows = cotangent.reshape(cell_count, channels)
    contract_rows = (((0,), (0,)), ((), ()))
    contract_cols = (((1,), (1,)), ((), ()))
    w_out_grad = lax.dot_general(
        activated, target_rows, contract_rows, preferred_element_type=jnp.float32
    )
    act_grad = lax.dot_general(
        target_rows, w_out, contract_cols, preferred_element_type=jnp.float32
    )
    pre_grad = (act_grad * sigmoid_pre * (1.0 + pre_act * (1.0 - sigmoid_pre))).astype(jnp.bfloat16)
    w_in_grad = lax.dot_general(
        hidden_in, pre_grad, contract_rows, preferred_element_type=jnp.float32
    )
    w_in_grad, w_out_grad, pre_grad = lax.optimization_barrier((w_in_grad, w_out_grad, pre_grad))
    hidden_grad = lax.dot_general(pre_grad, w_in, contract_cols, preferred_element_type=jnp.float32)
    gain_grad = jnp.sum(hidden_grad * normalized, axis=0)
    w_in_grad, w_out_grad = lax.psum((w_in_grad, w_out_grad), ("face", "row", "col"))
    scaled_grad = hidden_grad * gain_float
    aggregated_grad = inverse_rms * (
        scaled_grad - normalized * jnp.mean(scaled_grad * normalized, axis=-1, keepdims=True)
    )
    aggregated_grad = aggregated_grad.reshape(local_count, rows_dev, cols_dev, channels)
    stencil_grad = stencil_backward(offsets, extended, aggregated_grad)
    tap_count = stencil_grad.shape[0]
    small_grads = jnp.concatenate([stencil_grad, gain_grad[None, :]], axis=0)
    small_grads, increment = lax.optimization_barrier((small_grads, increment))
    small_grads = butterfly_sum(small_grads, ("face", "row", "col"))
    stencil_grad = small_grads[:tap_count]
    gain_grad = small_grads[tap_count]
    return (increment.reshape(state.shape), stencil_grad, gain_grad, w_in_grad, w_out_grad)


def butterfly_sum(value, axes):
    for axis in axes:
        count = lax.axis_size(axis)
        if count & (count - 1):
            value = lax.psum(value, axis)
            continue
        step = 1
        while step < count:
            value = value + lax.ppermute(value, axis, [(i, i ^ step) for i in range(count)])
            step *= 2
    return value


def solution(mesh):
    in_specs = (
        P("face", "row", "col", None),
        P(),
        P(),
        P(),
        P(),
        P(),
        P(),
        P("face", "row", "col", None),
    )
    out_specs = (P("face", "row", "col", None), P(), P(), P(), P())
    return jax.shard_map(shards, mesh=mesh, in_specs=in_specs, out_specs=out_specs, check_vma=False)
```
